256 devices in a mesh: gz: 32 (over x, z_hi, core), gy: 8 (over y, z_lo).
Axes of the slice: x: 4, y: 4, z: 8 (z_hi: 4, z_lo: 2; z = z_hi * 2 + z_lo), core: 2. Of those that a mesh axis runs over, the one named last changes fastest.
Arguments:
- saved_order_parameter: float32 [256, 128, 512], P('gz', 'gy'), may hold values from 0 to 1
- saved_heat_level: float32 [256, 128, 512], P('gz', 'gy'), may hold values from 0 to 1.5
- kinetic_rate_field: float32 [256, 128, 512], P('gz', 'gy'), may hold values from 0.5 to 2
- order_parameter_adjoint_seed: float32 [256, 128, 512], P('gz', 'gy'), may hold values from -6 to 6
- heat_level_adjoint_seed: float32 [256, 128, 512], P('gz', 'gy'), may hold values from -6 to 6
Outputs:
- start_phase: float32 [256, 128, 512], P('gz', 'gy')
- start_temp: float32 [256, 128, 512], P('gz', 'gy')
- grad_mobility: float32 [256, 128, 512], P('gz', 'gy')
The draws below stay inside these ranges and needn't reach their ends.
All inputs are finite; a program needn't handle non-finite values.
Results may differ from the reference program's by a relative error of at most 0.00002.
Values sent between devices are 32-bit elements; how exact they have to be, the bound alone decides.
No kernel may reach another device: no remote copies, remote signals or barrier semaphores. Data moves between devices by JAX's collectives and lax.ppermute only.
A program may use at most 64 MiB of HBM per device.

```python
import math
import jax
import jax.numpy as jnp

GRID_LENGTH_EAST = 512
GRID_LENGTH_UPWARD = 256
GRID_LENGTH_NORTH = 128


def level_of(stream_key, extent, pieces, smallest, top_value):
    loudness, own = 1.0, jax.random.fold_in(stream_key, 6)
    for position, shards_of in pieces:
        heights = jnp.exp(jax.random.uniform(jax.random.fold_in(own, position), (shards_of,), jnp.float32, smallest / len(pieces), top_value / len(pieces)))
        loudness = loudness * jnp.repeat(heights, extent[position] // shards_of).reshape([-1 if axis == position else 1 for axis in range(len(extent))])
    return loudness


def scatter_about(rng, extent, width, bound, pieces=(), kind=jnp.bfloat16):
    drawn = width * jax.random.normal(rng, extent, jnp.float32)
    if pieces:
        drawn = drawn * level_of(rng, extent, pieces, -0.22, 0.18)
    return jnp.clip(drawn, -bound, bound).astype(kind)


def setup_inputs(seed: int = 0) -> dict:
    arg_keys = jax.random.split(jax.random.key(seed), 6)
    saved_order_parameter = jnp.clip(1.0 * jax.random.uniform(arg_keys[0], (GRID_LENGTH_UPWARD, GRID_LENGTH_NORTH, GRID_LENGTH_EAST), jnp.float32) ** level_of(arg_keys[0], (GRID_LENGTH_UPWARD, GRID_LENGTH_NORTH, GRID_LENGTH_EAST), ((0, 32), (1, 8)), -0.2, 0.2), 0.0, 1.0)
    saved_heat_level = jnp.clip(1.5 * jax.random.uniform(arg_keys[1], (GRID_LENGTH_UPWARD, GRID_LENGTH_NORTH, GRID_LENGTH_EAST), jnp.float32) ** level_of(arg_keys[1], (GRID_LENGTH_UPWARD, GRID_LENGTH_NORTH, GRID_LENGTH_EAST), ((0, 32), (1, 8)), -0.2, 0.2), 0.0, 1.5)
    kinetic_rate_field = jnp.clip(jnp.exp(math.log(2.0) - 1.3862944 * jax.random.uniform(arg_keys[2], (GRID_LENGTH_UPWARD, GRID_LENGTH_NORTH, GRID_LENGTH_EAST), jnp.float32) ** level_of(arg_keys[2], (GRID_LENGTH_UPWARD, GRID_LENGTH_NORTH, GRID_LENGTH_EAST), ((0, 32), (1, 8)), -0.2, 0.2)), 0.5, 2.0)
    order_parameter_adjoint_seed = scatter_about(arg_keys[3], (GRID_LENGTH_UPWARD, GRID_LENGTH_NORTH, GRID_LENGTH_EAST), 1.0, 6.0, ((0, 32), (1, 8)), jnp.float32)
    heat_level_adjoint_seed = scatter_about(arg_keys[4], (GRID_LENGTH_UPWARD, GRID_LENGTH_NORTH, GRID_LENGTH_EAST), 1.0, 6.0, ((0, 32), (1, 8)), jnp.float32)
    return {"saved_order_parameter": saved_order_parameter, "saved_heat_level": saved_heat_level, "kinetic_rate_field": kinetic_rate_field, "order_parameter_adjoint_seed": order_parameter_adjoint_seed, "heat_level_adjoint_seed": heat_level_adjoint_seed}


TIME_STEP = 0.15
ENERGY_SCALE = 0.5
ANISOTROPY = 0.05
GRAD_FLOOR = 0.01
LATENT_HEAT = 1.8
DRIVE_SCALE = 0.9
DRIVE_SHARP = 10.0
MELT_POINT = 1.0

def advance_solver_step(phase_wide, temp_wide, kinetic_rate_field):
    padded = jnp.pad(phase_wide, ((0, 0), (0, 0), (2, 2)))
    grad_z = 0.5 * (padded[2:, 1:-1, 1:-1] - padded[:-2, 1:-1, 1:-1])
    grad_y = 0.5 * (padded[1:-1, 2:, 1:-1] - padded[1:-1, :-2, 1:-1])
    grad_x = 0.5 * (padded[1:-1, 1:-1, 2:] - padded[1:-1, 1:-1, :-2])
    sq_z = grad_z * grad_z
    sq_y = grad_y * grad_y
    sq_x = grad_x * grad_x
    squared = sq_z + sq_y + sq_x + GRAD_FLOOR
    quartic = (sq_z * sq_z + sq_y * sq_y + sq_x * sq_x) / (squared * squared)
    anisotropy = 1.0 + ANISOTROPY * (4.0 * quartic - 3.0)
    aniso_sq = anisotropy * anisotropy
    factor_a = 16.0 * ANISOTROPY * anisotropy / squared
    flux_z = ENERGY_SCALE * (aniso_sq * grad_z + factor_a * grad_z * (sq_z - quartic * squared))
    flux_y = ENERGY_SCALE * (aniso_sq * grad_y + factor_a * grad_y * (sq_y - quartic * squared))
    flux_x = ENERGY_SCALE * (aniso_sq * grad_x + factor_a * grad_x * (sq_x - quartic * squared))
    divergence = 0.5 * (flux_z[2:, 1:-1, 1:-1] - flux_z[:-2, 1:-1, 1:-1])
    divergence = divergence + 0.5 * (flux_y[1:-1, 2:, 1:-1] - flux_y[1:-1, :-2, 1:-1])
    divergence = divergence + 0.5 * (flux_x[1:-1, 1:-1, 2:] - flux_x[1:-1, 1:-1, :-2])
    phase_now = phase_wide[2:-2, 2:-2]
    temp_now = temp_wide[2:-2, 2:-2]
    driving = DRIVE_SCALE / jnp.pi * jnp.arctan(DRIVE_SHARP * (MELT_POINT - temp_now))
    growth = kinetic_rate_field * (divergence + phase_now * (1.0 - phase_now) * (phase_now - 0.5 + driving))
    new_phase = phase_now + TIME_STEP * growth
    temp_x = jnp.pad(temp_now, ((0, 0), (0, 0), (1, 1)))
    laplacian = temp_wide[3:-1, 2:-2] + temp_wide[1:-3, 2:-2] + temp_wide[2:-2, 3:-1] + temp_wide[2:-2, 1:-3]
    laplacian = laplacian + temp_x[:, :, 2:] + temp_x[:, :, :-2] - 6.0 * temp_now
    new_temp = temp_now + TIME_STEP * laplacian + LATENT_HEAT * (new_phase - phase_now)
    return (new_phase, new_temp)

def widen_slices(field):
    return jnp.pad(field, ((2, 2), (2, 2), (0, 0)))

def advance_mapping(saved_order_parameter, saved_heat_level, kinetic_rate_field):
    return advance_solver_step(widen_slices(saved_order_parameter), widen_slices(saved_heat_level), kinetic_rate_field)

def reference(saved_order_parameter, saved_heat_level, kinetic_rate_field, order_parameter_adjoint_seed, heat_level_adjoint_seed):
    succeeding_order_parameter, succeeding_heat_level = advance_mapping(saved_order_parameter, saved_heat_level, kinetic_rate_field)
    discarded_result, sensitivity_latest = jax.vjp(advance_mapping, succeeding_order_parameter, succeeding_heat_level, kinetic_rate_field)
    halfway_order_parameter, halfway_heat_level, latest_kinetic_rate = sensitivity_latest((order_parameter_adjoint_seed, heat_level_adjoint_seed))
    discarded_result, prior_backward_sweep = jax.vjp(advance_mapping, saved_order_parameter, saved_heat_level, kinetic_rate_field)
    start_phase, start_temp, early_mob = prior_backward_sweep((halfway_order_parameter, halfway_heat_level))
    return (start_phase, start_temp, latest_kinetic_rate + early_mob)
```

```python
import jax
import jax.numpy as jnp
from jax import lax
from jax.sharding import PartitionSpec as P

TIME_STEP = 0.15
ENERGY_SCALE = 0.5
ANISOTROPY = 0.05
GRAD_FLOOR = 0.01
LATENT_HEAT = 1.8
DRIVE_SCALE = 0.9
DRIVE_SHARP = 10.0
MELT_POINT = 1.0


def from_behind(block, axis, distance):
    devices = range(lax.axis_size(axis))
    route = [(i - distance, i) for i in devices if i - distance in devices]
    return lax.ppermute(block, axis, route)


def extended(cells, sides, width):
    for axis, dim in sides:
        count = lax.axis_size(axis)
        ends = count - 1
        head = lax.slice_in_dim(cells, 0, width, axis=dim)
        tail = lax.slice_in_dim(cells, cells.shape[dim] - width, cells.shape[dim], axis=dim)
        cells = jnp.concatenate(
            [
                lax.ppermute(tail, axis, [(i, (i + 1) % count) for i in range(ends)]),
                cells,
                lax.ppermute(head, axis, [((i + 1) % count, i) for i in range(ends)]),
            ],
            axis=dim,
        )
    return cells


def advance_solver_step(phase_wide, temp_wide, kinetic_rate_field):
    padded = jnp.pad(phase_wide, ((0, 0), (0, 0), (2, 2)))
    grad_z = 0.5 * (padded[2:, 1:-1, 1:-1] - padded[:-2, 1:-1, 1:-1])
    grad_y = 0.5 * (padded[1:-1, 2:, 1:-1] - padded[1:-1, :-2, 1:-1])
    grad_x = 0.5 * (padded[1:-1, 1:-1, 2:] - padded[1:-1, 1:-1, :-2])
    sq_z = grad_z * grad_z
    sq_y = grad_y * grad_y
    sq_x = grad_x * grad_x
    squared = sq_z + sq_y + sq_x + GRAD_FLOOR
    quartic = (sq_z * sq_z + sq_y * sq_y + sq_x * sq_x) / (squared * squared)
    anisotropy = 1.0 + ANISOTROPY * (4.0 * quartic - 3.0)
    aniso_sq = anisotropy * anisotropy
    factor_a = 16.0 * ANISOTROPY * anisotropy / squared
    flux_z = ENERGY_SCALE * (aniso_sq * grad_z + factor_a * grad_z * (sq_z - quartic * squared))
    flux_y = ENERGY_SCALE * (aniso_sq * grad_y + factor_a * grad_y * (sq_y - quartic * squared))
    flux_x = ENERGY_SCALE * (aniso_sq * grad_x + factor_a * grad_x * (sq_x - quartic * squared))
    divergence = 0.5 * (flux_z[2:, 1:-1, 1:-1] - flux_z[:-2, 1:-1, 1:-1])
    divergence = divergence + 0.5 * (flux_y[1:-1, 2:, 1:-1] - flux_y[1:-1, :-2, 1:-1])
    divergence = divergence + 0.5 * (flux_x[1:-1, 1:-1, 2:] - flux_x[1:-1, 1:-1, :-2])
    phase_now = phase_wide[2:-2, 2:-2]
    temp_now = temp_wide[2:-2, 2:-2]
    driving = DRIVE_SCALE / jnp.pi * jnp.arctan(DRIVE_SHARP * (MELT_POINT - temp_now))
    growth = kinetic_rate_field * (
        divergence + phase_now * (1.0 - phase_now) * (phase_now - 0.5 + driving)
    )
    new_phase = phase_now + TIME_STEP * growth
    temp_x = jnp.pad(temp_now, ((0, 0), (0, 0), (1, 1)))
    laplacian = (
        temp_wide[3:-1, 2:-2]
        + temp_wide[1:-3, 2:-2]
        + temp_wide[2:-2, 3:-1]
        + temp_wide[2:-2, 1:-3]
    )
    laplacian = laplacian + temp_x[:, :, 2:] + temp_x[:, :, :-2] - 6.0 * temp_now
    new_temp = temp_now + TIME_STEP * laplacian + LATENT_HEAT * (new_phase - phase_now)
    return (new_phase, new_temp)


def fold_rims(sensitivity_order_parameter, sensitivity_heat_level):
    stacked = jnp.stack((sensitivity_order_parameter, sensitivity_heat_level))
    lower_rim = stacked[:, :2]
    upper_rim = stacked[:, -2:]
    middle = stacked[:, 2:-2]
    from_above = from_behind(lower_rim, "gz", -1)
    from_below = from_behind(upper_rim, "gz", 1)
    middle = jnp.concatenate(
        (middle[:, :2] + from_below, middle[:, 2:-2], middle[:, -2:] + from_above), axis=1
    )
    lower_rim = middle[:, :, :2]
    upper_rim = middle[:, :, -2:]
    middle = middle[:, :, 2:-2]
    from_above = from_behind(lower_rim, "gy", -1)
    from_below = from_behind(upper_rim, "gy", 1)
    middle = jnp.concatenate(
        (middle[:, :, :2] + from_below, middle[:, :, 2:-2], middle[:, :, -2:] + from_above), axis=2
    )
    return (middle[0], middle[1])


def inside_grid(cells, margin):
    nz, ny = cells.shape[0] - 2 * margin, cells.shape[1] - 2 * margin
    z = lax.axis_index("gz") * nz - margin + lax.broadcasted_iota(jnp.int32, cells.shape, 0)
    y = lax.axis_index("gy") * ny - margin + lax.broadcasted_iota(jnp.int32, cells.shape, 1)
    total_z = nz * lax.axis_size("gz")
    total_y = ny * lax.axis_size("gy")
    return (z >= 0) & (z < total_z) & (y >= 0) & (y < total_y)


def body(
    saved_order_parameter,
    saved_heat_level,
    kinetic_rate_field,
    order_parameter_adjoint_seed,
    heat_level_adjoint_seed,
):
    state = extended(
        jnp.stack((saved_order_parameter, saved_heat_level, kinetic_rate_field)),
        (("gz", 1), ("gy", 2)),
        6,
    )
    seeds = extended(
        jnp.stack((order_parameter_adjoint_seed, heat_level_adjoint_seed)),
        (("gz", 1), ("gy", 2)),
        2,
    )
    phase_wide, temp_wide, rate_wide = state[0], state[1], state[2]
    succeeding_order_parameter, succeeding_heat_level = advance_solver_step(
        phase_wide, temp_wide, rate_wide[2:-2, 2:-2]
    )
    valid = inside_grid(succeeding_order_parameter, 4)
    succeeding_order_parameter = jnp.where(valid, succeeding_order_parameter, 0.0)
    succeeding_heat_level = jnp.where(valid, succeeding_heat_level, 0.0)
    discarded_result, sensitivity_latest = jax.vjp(
        advance_solver_step,
        succeeding_order_parameter,
        succeeding_heat_level,
        rate_wide[4:-4, 4:-4],
    )
    sensitivity_order_parameter, sensitivity_heat_level, latest_kinetic_rate = sensitivity_latest(
        (seeds[0], seeds[1])
    )
    halfway_order_parameter = sensitivity_order_parameter[4:-4, 4:-4]
    halfway_heat_level = sensitivity_heat_level[4:-4, 4:-4]
    latest_kinetic_rate = latest_kinetic_rate[2:-2, 2:-2]
    discarded_result, prior_backward_sweep = jax.vjp(
        advance_solver_step,
        phase_wide[4:-4, 4:-4],
        temp_wide[4:-4, 4:-4],
        rate_wide[6:-6, 6:-6],
    )
    sensitivity_order_parameter, sensitivity_heat_level, early_mob = prior_backward_sweep(
        (halfway_order_parameter, halfway_heat_level)
    )
    start_phase, start_temp = fold_rims(sensitivity_order_parameter, sensitivity_heat_level)
    return (start_phase, start_temp, latest_kinetic_rate + early_mob)


def solution(mesh):
    return jax.shard_map(
        body,
        mesh=mesh,
        in_specs=(
            P("gz", "gy", None),
            P("gz", "gy", None),
            P("gz", "gy", None),
            P("gz", "gy", None),
            P("gz", "gy", None),
        ),
        out_specs=(P("gz", "gy", None), P("gz", "gy", None), P("gz", "gy", None)),
        check_vma=False,
    )
```

```python
import jax
import jax.numpy as jnp
from jax import lax
from jax.sharding import PartitionSpec as P

TIME_STEP = 0.15
ENERGY_SCALE = 0.5
ANISOTROPY = 0.05
GRAD_FLOOR = 0.01
LATENT_HEAT = 1.8
DRIVE_SCALE = 0.9
DRIVE_SHARP = 10.0
MELT_POINT = 1.0


def from_behind(block, axis, distance):
    devices = range(lax.axis_size(axis))
    route = [(i - distance, i) for i in devices if i - distance in devices]
    return lax.ppermute(block, axis, route)


def extended(cells, sides, width):
    for axis, dim in sides:
        count = lax.axis_size(axis)
        ends = count - 1
        head = lax.slice_in_dim(cells, 0, width, axis=dim)
        tail = lax.slice_in_dim(cells, cells.shape[dim] - width, cells.shape[dim], axis=dim)
        cells = jnp.concatenate(
            [
                lax.ppermute(tail, axis, [(i, (i + 1) % count) for i in range(ends)]),
                cells,
                lax.ppermute(head, axis, [((i + 1) % count, i) for i in range(ends)]),
            ],
            axis=dim,
        )
    return cells


def advance_solver_step(phase_wide, temp_wide, kinetic_rate_field):
    padded = jnp.pad(phase_wide, ((0, 0), (0, 0), (2, 2)))
    grad_z = 0.5 * (padded[2:, 1:-1, 1:-1] - padded[:-2, 1:-1, 1:-1])
    grad_y = 0.5 * (padded[1:-1, 2:, 1:-1] - padded[1:-1, :-2, 1:-1])
    grad_x = 0.5 * (padded[1:-1, 1:-1, 2:] - padded[1:-1, 1:-1, :-2])
    sq_z = grad_z * grad_z
    sq_y = grad_y * grad_y
    sq_x = grad_x * grad_x
    squared = sq_z + sq_y + sq_x + GRAD_FLOOR
    quartic = (sq_z * sq_z + sq_y * sq_y + sq_x * sq_x) / (squared * squared)
    anisotropy = 1.0 + ANISOTROPY * (4.0 * quartic - 3.0)
    aniso_sq = anisotropy * anisotropy
    factor_a = 16.0 * ANISOTROPY * anisotropy / squared
    flux_z = ENERGY_SCALE * (aniso_sq * grad_z + factor_a * grad_z * (sq_z - quartic * squared))
    flux_y = ENERGY_SCALE * (aniso_sq * grad_y + factor_a * grad_y * (sq_y - quartic * squared))
    flux_x = ENERGY_SCALE * (aniso_sq * grad_x + factor_a * grad_x * (sq_x - quartic * squared))
    divergence = 0.5 * (flux_z[2:, 1:-1, 1:-1] - flux_z[:-2, 1:-1, 1:-1])
    divergence = divergence + 0.5 * (flux_y[1:-1, 2:, 1:-1] - flux_y[1:-1, :-2, 1:-1])
    divergence = divergence + 0.5 * (flux_x[1:-1, 1:-1, 2:] - flux_x[1:-1, 1:-1, :-2])
    phase_now = phase_wide[2:-2, 2:-2]
    temp_now = temp_wide[2:-2, 2:-2]
    driving = DRIVE_SCALE / jnp.pi * jnp.arctan(DRIVE_SHARP * (MELT_POINT - temp_now))
    growth = kinetic_rate_field * (
        divergence + phase_now * (1.0 - phase_now) * (phase_now - 0.5 + driving)
    )
    new_phase = phase_now + TIME_STEP * growth
    temp_x = jnp.pad(temp_now, ((0, 0), (0, 0), (1, 1)))
    laplacian = (
        temp_wide[3:-1, 2:-2]
        + temp_wide[1:-3, 2:-2]
        + temp_wide[2:-2, 3:-1]
        + temp_wide[2:-2, 1:-3]
    )
    laplacian = laplacian + temp_x[:, :, 2:] + temp_x[:, :, :-2] - 6.0 * temp_now
    new_temp = temp_now + TIME_STEP * laplacian + LATENT_HEAT * (new_phase - phase_now)
    return (new_phase, new_temp)


def fold_rims(contributions, width, sides):
    for axis, dim in sides:
        size = contributions.shape[dim]
        lower_rim = lax.slice_in_dim(contributions, 0, width, axis=dim)
        upper_rim = lax.slice_in_dim(contributions, size - width, size, axis=dim)
        middle = lax.slice_in_dim(contributions, width, size - width, axis=dim)
        inner = size - 2 * width
        lower_rim, upper_rim = lax.optimization_barrier((lower_rim, upper_rim))
        from_above = from_behind(lower_rim, axis, -1)
        from_below = from_behind(upper_rim, axis, 1)
        contributions = jnp.concatenate(
            (
                lax.slice_in_dim(middle, 0, width, axis=dim) + from_below,
                lax.slice_in_dim(middle, width, inner - width, axis=dim),
                lax.slice_in_dim(middle, inner - width, inner, axis=dim) + from_above,
            ),
            axis=dim,
        )
    return contributions


def inside_grid(cells, margin):
    nz, ny = cells.shape[0] - 2 * margin, cells.shape[1] - 2 * margin
    z = lax.axis_index("gz") * nz - margin + lax.broadcasted_iota(jnp.int32, cells.shape, 0)
    y = lax.axis_index("gy") * ny - margin + lax.broadcasted_iota(jnp.int32, cells.shape, 1)
    total_z = nz * lax.axis_size("gz")
    total_y = ny * lax.axis_size("gy")
    return (z >= 0) & (z < total_z) & (y >= 0) & (y < total_y)


def body(
    saved_order_parameter,
    saved_heat_level,
    kinetic_rate_field,
    order_parameter_adjoint_seed,
    heat_level_adjoint_seed,
):
    state = extended(
        jnp.stack((saved_order_parameter, saved_heat_level, kinetic_rate_field)),
        (("gz", 1), ("gy", 2)),
        4,
    )
    phase_wide, temp_wide, rate_wide = state[0], state[1], state[2]
    succeeding_order_parameter, succeeding_heat_level = advance_solver_step(
        phase_wide, temp_wide, rate_wide[2:-2, 2:-2]
    )
    valid = inside_grid(succeeding_order_parameter, 2)
    succeeding_order_parameter = jnp.where(valid, succeeding_order_parameter, 0.0)
    succeeding_heat_level = jnp.where(valid, succeeding_heat_level, 0.0)
    discarded_result, sensitivity_latest = jax.vjp(
        advance_solver_step,
        succeeding_order_parameter,
        succeeding_heat_level,
        rate_wide[4:-4, 4:-4],
    )
    halfway_order_parameter, halfway_heat_level, latest_kinetic_rate = sensitivity_latest(
        (order_parameter_adjoint_seed, heat_level_adjoint_seed)
    )
    halfway_order_parameter = jnp.where(valid, halfway_order_parameter, 0.0)
    halfway_heat_level = jnp.where(valid, halfway_heat_level, 0.0)
    discarded_result, prior_backward_sweep = jax.vjp(
        advance_solver_step, phase_wide, temp_wide, rate_wide[2:-2, 2:-2]
    )
    sensitivity_order_parameter, sensitivity_heat_level, early_mob = prior_backward_sweep(
        (halfway_order_parameter, halfway_heat_level)
    )
    early_mob = jnp.pad(early_mob, ((2, 2), (2, 2), (0, 0)))
    folded = fold_rims(
        jnp.stack((sensitivity_order_parameter, sensitivity_heat_level, early_mob)),
        4,
        (("gy", 2), ("gz", 1)),
    )
    return (folded[0], folded[1], latest_kinetic_rate + folded[2])


def solution(mesh):
    return jax.shard_map(
        body,
        mesh=mesh,
        in_specs=(
            P("gz", "gy", None),
            P("gz", "gy", None),
            P("gz", "gy", None),
            P("gz", "gy", None),
            P("gz", "gy", None),
        ),
        out_specs=(P("gz", "gy", None), P("gz", "gy", None), P("gz", "gy", None)),
        check_vma=False,
    )
```

```python
import jax
import jax.numpy as jnp
from jax import lax
from jax.sharding import PartitionSpec as P

TIME_STEP = 0.15
ENERGY_SCALE = 0.5
ANISOTROPY = 0.05
GRAD_FLOOR = 0.01
LATENT_HEAT = 1.8
DRIVE_SCALE = 0.9
DRIVE_SHARP = 10.0
MELT_POINT = 1.0


def from_behind(block, axis, distance):
    devices = range(lax.axis_size(axis))
    route = [(i - distance, i) for i in devices if i - distance in devices]
    return lax.ppermute(block, axis, route)


def swap_rims(fields, widths, axis, dim):
    lower = [lax.slice_in_dim(f, 0, w, axis=dim) for f, w in zip(fields, widths)]
    upper = [
        lax.slice_in_dim(f, f.shape[dim] - w, f.shape[dim], axis=dim)
        for f, w in zip(fields, widths)
    ]
    lower, upper = jnp.concatenate(lower, 0), jnp.concatenate(upper, 0)
    lower, upper = lax.optimization_barrier((lower, upper))
    from_above = from_behind(lower, axis, -1)
    from_below = from_behind(upper, axis, 1)
    sizes = [r.shape[0] for r in (lax.slice_in_dim(f, 0, w, axis=dim) for f, w in zip(fields, widths))]
    cuts = [sum(sizes[:i]) for i in range(len(sizes) + 1)]
    below = [from_below[cuts[i]:cuts[i + 1]] for i in range(len(sizes))]
    above = [from_above[cuts[i]:cuts[i + 1]] for i in range(len(sizes))]
    return below, above


def extended(fields, widths, axis, dim):
    below, above = swap_rims(fields, widths, axis, dim)
    return [jnp.concatenate((b, f, a), axis=dim) for f, b, a in zip(fields, below, above)]


def folded(fields, widths, axis, dim):
    below, above = swap_rims(fields, widths, axis, dim)
    result = []
    for f, w, b, a in zip(fields, widths, below, above):
        size = f.shape[dim]
        result.append(
            jnp.concatenate(
                (
                    lax.slice_in_dim(f, w, 2 * w, axis=dim) + b,
                    lax.slice_in_dim(f, 2 * w, size - 2 * w, axis=dim),
                    lax.slice_in_dim(f, size - 2 * w, size - w, axis=dim) + a,
                ),
                axis=dim,
            )
        )
    return result


def advance_solver_step(phase_wide, temp_ring, kinetic_rate_field):
    padded = jnp.pad(phase_wide, ((0, 0), (0, 0), (2, 2)))
    grad_z = 0.5 * (padded[2:, 1:-1, 1:-1] - padded[:-2, 1:-1, 1:-1])
    grad_y = 0.5 * (padded[1:-1, 2:, 1:-1] - padded[1:-1, :-2, 1:-1])
    grad_x = 0.5 * (padded[1:-1, 1:-1, 2:] - padded[1:-1, 1:-1, :-2])
    sq_z = grad_z * grad_z
    sq_y = grad_y * grad_y
    sq_x = grad_x * grad_x
    squared = sq_z + sq_y + sq_x + GRAD_FLOOR
    quartic = (sq_z * sq_z + sq_y * sq_y + sq_x * sq_x) / (squared * squared)
    anisotropy = 1.0 + ANISOTROPY * (4.0 * quartic - 3.0)
    aniso_sq = anisotropy * anisotropy
    factor_a = 16.0 * ANISOTROPY * anisotropy / squared
    flux_z = ENERGY_SCALE * (aniso_sq * grad_z + factor_a * grad_z * (sq_z - quartic * squared))
    flux_y = ENERGY_SCALE * (aniso_sq * grad_y + factor_a * grad_y * (sq_y - quartic * squared))
    flux_x = ENERGY_SCALE * (aniso_sq * grad_x + factor_a * grad_x * (sq_x - quartic * squared))
    divergence = 0.5 * (flux_z[2:, 1:-1, 1:-1] - flux_z[:-2, 1:-1, 1:-1])
    divergence = divergence + 0.5 * (flux_y[1:-1, 2:, 1:-1] - flux_y[1:-1, :-2, 1:-1])
    divergence = divergence + 0.5 * (flux_x[1:-1, 1:-1, 2:] - flux_x[1:-1, 1:-1, :-2])
    phase_now = phase_wide[2:-2, 2:-2]
    temp_now = temp_ring[1:-1, 1:-1]
    driving = DRIVE_SCALE / jnp.pi * jnp.arctan(DRIVE_SHARP * (MELT_POINT - temp_now))
    growth = kinetic_rate_field * (
        divergence + phase_now * (1.0 - phase_now) * (phase_now - 0.5 + driving)
    )
    new_phase = phase_now + TIME_STEP * growth
    temp_x = jnp.pad(temp_now, ((0, 0), (0, 0), (1, 1)))
    laplacian = (
        temp_ring[2:, 1:-1]
        + temp_ring[:-2, 1:-1]
        + temp_ring[1:-1, 2:]
        + temp_ring[1:-1, :-2]
    )
    laplacian = laplacian + temp_x[:, :, 2:] + temp_x[:, :, :-2] - 6.0 * temp_now
    new_temp = temp_now + TIME_STEP * laplacian + LATENT_HEAT * (new_phase - phase_now)
    return (new_phase, new_temp)


def inside_grid(cells, margin):
    nz, ny = cells.shape[0] - 2 * margin, cells.shape[1] - 2 * margin
    z = lax.axis_index("gz") * nz - margin + lax.broadcasted_iota(jnp.int32, cells.shape, 0)
    y = lax.axis_index("gy") * ny - margin + lax.broadcasted_iota(jnp.int32, cells.shape, 1)
    total_z = nz * lax.axis_size("gz")
    total_y = ny * lax.axis_size("gy")
    return (z >= 0) & (z < total_z) & (y >= 0) & (y < total_y)


def ring(cells, width):
    return jnp.pad(cells, ((width, width), (width, width), (0, 0)))


def body(
    saved_order_parameter,
    saved_heat_level,
    kinetic_rate_field,
    order_parameter_adjoint_seed,
    heat_level_adjoint_seed,
):
    fields = extended(
        [saved_order_parameter, saved_heat_level, kinetic_rate_field], [4, 3, 2], "gz", 0
    )
    phase_wide, temp_wide, rate_wide = extended(fields, [4, 4, 4], "gy", 1)
    temp_wide = temp_wide[:, 1:-1]
    rate_wide = rate_wide[:, 2:-2]
    (succeeding_order_parameter, succeeding_heat_level), prior_backward_sweep = jax.vjp(
        advance_solver_step, phase_wide, temp_wide, rate_wide
    )
    valid = inside_grid(succeeding_order_parameter, 2)
    succeeding_order_parameter = jnp.where(valid, succeeding_order_parameter, 0.0)
    succeeding_heat_level = jnp.where(valid, succeeding_heat_level, 0.0)
    discarded_result, sensitivity_latest = jax.vjp(
        advance_solver_step,
        succeeding_order_parameter,
        succeeding_heat_level[1:-1, 1:-1],
        rate_wide[2:-2, 2:-2],
    )
    halfway_order_parameter, halfway_heat_level, latest_kinetic_rate = sensitivity_latest(
        (order_parameter_adjoint_seed, heat_level_adjoint_seed)
    )
    halfway_heat_level = ring(halfway_heat_level, 1)
    halfway_order_parameter = jnp.where(valid, halfway_order_parameter, 0.0)
    halfway_heat_level = jnp.where(valid, halfway_heat_level, 0.0)
    sensitivity_order_parameter, sensitivity_heat_level, early_mob = prior_backward_sweep(
        (halfway_order_parameter, halfway_heat_level)
    )
    fields = folded(
        [
            sensitivity_order_parameter,
            jnp.pad(sensitivity_heat_level, ((0, 0), (1, 1), (0, 0))),
            jnp.pad(early_mob, ((0, 0), (2, 2), (0, 0))),
        ],
        [4, 4, 4],
        "gy",
        1,
    )
    start_phase, start_temp, early_mob = folded(fields, [4, 3, 2], "gz", 0)
    return (start_phase, start_temp, latest_kinetic_rate + early_mob)


def solution(mesh):
    return jax.shard_map(
        body,
        mesh=mesh,
        in_specs=(
            P("gz", "gy", None),
            P("gz", "gy", None),
            P("gz", "gy", None),
            P("gz", "gy", None),
            P("gz", "gy", None),
        ),
        out_specs=(P("gz", "gy", None), P("gz", "gy", None), P("gz", "gy", None)),
        check_vma=False,
    )
```

```python
import jax
import jax.numpy as jnp
from jax import lax
from jax.sharding import PartitionSpec as P

TIME_STEP = 0.15
ENERGY_SCALE = 0.5
ANISOTROPY = 0.05
GRAD_FLOOR = 0.01
LATENT_HEAT = 1.8
DRIVE_SCALE = 0.9
DRIVE_SHARP = 10.0
MELT_POINT = 1.0


def from_behind(block, axis, distance):
    devices = range(lax.axis_size(axis))
    route = [(i - distance, i) for i in devices if i - distance in devices]
    return lax.ppermute(block, axis, route)


def extended(cells, sides, width):
    for axis, dim in sides:
        count = lax.axis_size(axis)
        ends = count - 1
        head = lax.slice_in_dim(cells, 0, width, axis=dim)
        tail = lax.slice_in_dim(cells, cells.shape[dim] - width, cells.shape[dim], axis=dim)
        cells = jnp.concatenate(
            [
                lax.ppermute(tail, axis, [(i, (i + 1) % count) for i in range(ends)]),
                cells,
                lax.ppermute(head, axis, [((i + 1) % count, i) for i in range(ends)]),
            ],
            axis=dim,
        )
    return cells


def advance_solver_step(phase_wide, temp_wide, kinetic_rate_field):
    padded = jnp.pad(phase_wide, ((0, 0), (0, 0), (2, 2)))
    grad_z = 0.5 * (padded[2:, 1:-1, 1:-1] - padded[:-2, 1:-1, 1:-1])
    grad_y = 0.5 * (padded[1:-1, 2:, 1:-1] - padded[1:-1, :-2, 1:-1])
    grad_x = 0.5 * (padded[1:-1, 1:-1, 2:] - padded[1:-1, 1:-1, :-2])
    sq_z = grad_z * grad_z
    sq_y = grad_y * grad_y
    sq_x = grad_x * grad_x
    squared = sq_z + sq_y + sq_x + GRAD_FLOOR
    quartic = (sq_z * sq_z + sq_y * sq_y + sq_x * sq_x) / (squared * squared)
    anisotropy = 1.0 + ANISOTROPY * (4.0 * quartic - 3.0)
    aniso_sq = anisotropy * anisotropy
    factor_a = 16.0 * ANISOTROPY * anisotropy / squared
    flux_z = ENERGY_SCALE * (aniso_sq * grad_z + factor_a * grad_z * (sq_z - quartic * squared))
    flux_y = ENERGY_SCALE * (aniso_sq * grad_y + factor_a * grad_y * (sq_y - quartic * squared))
    flux_x = ENERGY_SCALE * (aniso_sq * grad_x + factor_a * grad_x * (sq_x - quartic * squared))
    divergence = 0.5 * (flux_z[2:, 1:-1, 1:-1] - flux_z[:-2, 1:-1, 1:-1])
    divergence = divergence + 0.5 * (flux_y[1:-1, 2:, 1:-1] - flux_y[1:-1, :-2, 1:-1])
    divergence = divergence + 0.5 * (flux_x[1:-1, 1:-1, 2:] - flux_x[1:-1, 1:-1, :-2])
    phase_now = phase_wide[2:-2, 2:-2]
    temp_now = temp_wide[2:-2, 2:-2]
    driving = DRIVE_SCALE / jnp.pi * jnp.arctan(DRIVE_SHARP * (MELT_POINT - temp_now))
    growth = kinetic_rate_field * (
        divergence + phase_now * (1.0 - phase_now) * (phase_now - 0.5 + driving)
    )
    new_phase = phase_now + TIME_STEP * growth
    temp_x = jnp.pad(temp_now, ((0, 0), (0, 0), (1, 1)))
    laplacian = (
        temp_wide[3:-1, 2:-2]
        + temp_wide[1:-3, 2:-2]
        + temp_wide[2:-2, 3:-1]
        + temp_wide[2:-2, 1:-3]
    )
    laplacian = laplacian + temp_x[:, :, 2:] + temp_x[:, :, :-2] - 6.0 * temp_now
    new_temp = temp_now + TIME_STEP * laplacian + LATENT_HEAT * (new_phase - phase_now)
    return (new_phase, new_temp)


def fold_rims(contributions, width, sides):
    for axis, dim in sides:
        size = contributions.shape[dim]
        lower_rim = lax.slice_in_dim(contributions, 0, width, axis=dim)
        upper_rim = lax.slice_in_dim(contributions, size - width, size, axis=dim)
        middle = lax.slice_in_dim(contributions, width, size - width, axis=dim)
        inner = size - 2 * width
        lower_rim, upper_rim = lax.optimization_barrier((lower_rim, upper_rim))
        from_above = from_behind(lower_rim, axis, -1)
        from_below = from_behind(upper_rim, axis, 1)
        contributions = jnp.concatenate(
            (
                lax.slice_in_dim(middle, 0, width, axis=dim) + from_below,
                lax.slice_in_dim(middle, width, inner - width, axis=dim),
                lax.slice_in_dim(middle, inner - width, inner, axis=dim) + from_above,
            ),
            axis=dim,
        )
    return contributions


def inside_grid(cells, margin):
    nz, ny = cells.shape[0] - 2 * margin, cells.shape[1] - 2 * margin
    z = lax.axis_index("gz") * nz - margin + lax.broadcasted_iota(jnp.int32, cells.shape, 0)
    y = lax.axis_index("gy") * ny - margin + lax.broadcasted_iota(jnp.int32, cells.shape, 1)
    total_z = nz * lax.axis_size("gz")
    total_y = ny * lax.axis_size("gy")
    return (z >= 0) & (z < total_z) & (y >= 0) & (y < total_y)


def adjoint_of_layers(first, last, state, seeds):
    phase_wide, temp_wide, rate_wide, succeeding_order_parameter, succeeding_heat_level, valid = state
    discarded_result, sensitivity_latest = jax.vjp(
        advance_solver_step,
        succeeding_order_parameter[first : last + 4],
        succeeding_heat_level[first : last + 4],
        rate_wide[4 + first : 4 + last, 4:-4],
    )
    halfway_order_parameter, halfway_heat_level, latest_kinetic_rate = sensitivity_latest(
        (seeds[0][first:last], seeds[1][first:last])
    )
    inside = valid[first : last + 4]
    halfway_order_parameter = jnp.where(inside, halfway_order_parameter, 0.0)
    halfway_heat_level = jnp.where(inside, halfway_heat_level, 0.0)
    discarded_result, prior_backward_sweep = jax.vjp(
        advance_solver_step,
        phase_wide[first : last + 8],
        temp_wide[first : last + 8],
        rate_wide[2 + first : 2 + last + 4, 2:-2],
    )
    sensitivity_order_parameter, sensitivity_heat_level, early_mob = prior_backward_sweep(
        (halfway_order_parameter, halfway_heat_level)
    )
    early_mob = jnp.pad(early_mob, ((2, 2), (2, 2), (0, 0)))
    contributions = jnp.stack((sensitivity_order_parameter, sensitivity_heat_level, early_mob))
    return contributions, latest_kinetic_rate


def body(
    saved_order_parameter,
    saved_heat_level,
    kinetic_rate_field,
    order_parameter_adjoint_seed,
    heat_level_adjoint_seed,
):
    state = extended(
        jnp.stack((saved_order_parameter, saved_heat_level, kinetic_rate_field)),
        (("gz", 1), ("gy", 2)),
        4,
    )
    phase_wide, temp_wide, rate_wide = state[0], state[1], state[2]
    succeeding_order_parameter, succeeding_heat_level = advance_solver_step(
        phase_wide, temp_wide, rate_wide[2:-2, 2:-2]
    )
    valid = inside_grid(succeeding_order_parameter, 2)
    succeeding_order_parameter = jnp.where(valid, succeeding_order_parameter, 0.0)
    succeeding_heat_level = jnp.where(valid, succeeding_heat_level, 0.0)
    state = (phase_wide, temp_wide, rate_wide, succeeding_order_parameter, succeeding_heat_level, valid)
    seeds = (order_parameter_adjoint_seed, heat_level_adjoint_seed)
    half = saved_order_parameter.shape[0] // 2
    lower, lower_rate = adjoint_of_layers(0, half, state, seeds)
    state, seeds, lower, lower_rate = lax.optimization_barrier((state, seeds, lower, lower_rate))
    lower = fold_rims(lower, 4, (("gy", 2),))
    upper, upper_rate = adjoint_of_layers(half, 2 * half, state, seeds)
    upper = fold_rims(upper, 4, (("gy", 2),))
    from_below = from_behind(upper[:, -4:], "gz", 1)
    from_above = from_behind(lower[:, :4], "gz", -1)
    total = lower[:, 4:] + upper[:, :-4]
    total = jnp.concatenate(
        (total[:, :4] + from_below, total[:, 4:-4], total[:, -4:] + from_above), axis=1
    )
    latest_kinetic_rate = jnp.concatenate((lower_rate, upper_rate), axis=0)
    return (total[0], total[1], latest_kinetic_rate + total[2])


def solution(mesh):
    return jax.shard_map(
        body,
        mesh=mesh,
        in_specs=(
            P("gz", "gy", None),
            P("gz", "gy", None),
            P("gz", "gy", None),
            P("gz", "gy", None),
            P("gz", "gy", None),
        ),
        out_specs=(P("gz", "gy", None), P("gz", "gy", None), P("gz", "gy", None)),
        check_vma=False,
    )
```

```python
import jax
import jax.numpy as jnp
from jax import lax
from jax.sharding import PartitionSpec as P

TIME_STEP = 0.15
ENERGY_SCALE = 0.5
ANISOTROPY = 0.05
GRAD_FLOOR = 0.01
LATENT_HEAT = 1.8
DRIVE_SCALE = 0.9
DRIVE_SHARP = 10.0
MELT_POINT = 1.0


def from_behind(block, axis, distance):
    devices = range(lax.axis_size(axis))
    route = [(i - distance, i) for i in devices if i - distance in devices]
    return lax.ppermute(block, axis, route)


def extended(cells, sides, width):
    for axis, dim in sides:
        count = lax.axis_size(axis)
        ends = count - 1
        head = lax.slice_in_dim(cells, 0, width, axis=dim)
        tail = lax.slice_in_dim(cells, cells.shape[dim] - width, cells.shape[dim], axis=dim)
        cells = jnp.concatenate(
            [
                lax.ppermute(tail, axis, [(i, (i + 1) % count) for i in range(ends)]),
                cells,
                lax.ppermute(head, axis, [((i + 1) % count, i) for i in range(ends)]),
            ],
            axis=dim,
        )
    return cells


def packed_z_halo(cells, widths):
    width, size = max(widths), cells.shape[1]
    tails = jnp.concatenate([cells[i, size - w :] for i, w in enumerate(widths)], 0)
    heads = jnp.concatenate([cells[i, :w] for i, w in enumerate(widths)], 0)
    from_below = from_behind(tails, "gz", 1)
    from_above = from_behind(heads, "gz", -1)
    cuts = [sum(widths[:i]) for i in range(len(widths) + 1)]
    below = jnp.stack(
        [
            jnp.pad(from_below[cuts[i] : cuts[i + 1]], ((width - w, 0), (0, 0), (0, 0)))
            for i, w in enumerate(widths)
        ]
    )
    above = jnp.stack(
        [
            jnp.pad(from_above[cuts[i] : cuts[i + 1]], ((0, width - w), (0, 0), (0, 0)))
            for i, w in enumerate(widths)
        ]
    )
    return jnp.concatenate((below, cells, above), axis=1)


def packed_z_fold(contributions, widths):
    width, size = max(widths), contributions.shape[1]
    lower = jnp.concatenate(
        [contributions[i, width - w : width] for i, w in enumerate(widths)], 0
    )
    upper = jnp.concatenate(
        [contributions[i, size - width : size - width + w] for i, w in enumerate(widths)], 0
    )
    lower, upper = lax.optimization_barrier((lower, upper))
    from_above = from_behind(lower, "gz", -1)
    from_below = from_behind(upper, "gz", 1)
    cuts = [sum(widths[:i]) for i in range(len(widths) + 1)]
    below = jnp.stack(
        [
            jnp.pad(from_below[cuts[i] : cuts[i + 1]], ((0, width - w), (0, 0), (0, 0)))
            for i, w in enumerate(widths)
        ]
    )
    above = jnp.stack(
        [
            jnp.pad(from_above[cuts[i] : cuts[i + 1]], ((width - w, 0), (0, 0), (0, 0)))
            for i, w in enumerate(widths)
        ]
    )
    middle = contributions[:, width : size - width]
    inner = size - 2 * width
    return jnp.concatenate(
        (
            middle[:, :width] + below,
            middle[:, width : inner - width],
            middle[:, inner - width :] + above,
        ),
        axis=1,
    )


def advance_solver_step(phase_wide, temp_wide, kinetic_rate_field):
    padded = jnp.pad(phase_wide, ((0, 0), (0, 0), (2, 2)))
    grad_z = 0.5 * (padded[2:, 1:-1, 1:-1] - padded[:-2, 1:-1, 1:-1])
    grad_y = 0.5 * (padded[1:-1, 2:, 1:-1] - padded[1:-1, :-2, 1:-1])
    grad_x = 0.5 * (padded[1:-1, 1:-1, 2:] - padded[1:-1, 1:-1, :-2])
    sq_z = grad_z * grad_z
    sq_y = grad_y * grad_y
    sq_x = grad_x * grad_x
    squared = sq_z + sq_y + sq_x + GRAD_FLOOR
    quartic = (sq_z * sq_z + sq_y * sq_y + sq_x * sq_x) / (squared * squared)
    anisotropy = 1.0 + ANISOTROPY * (4.0 * quartic - 3.0)
    aniso_sq = anisotropy * anisotropy
    factor_a = 16.0 * ANISOTROPY * anisotropy / squared
    flux_z = ENERGY_SCALE * (aniso_sq * grad_z + factor_a * grad_z * (sq_z - quartic * squared))
    flux_y = ENERGY_SCALE * (aniso_sq * grad_y + factor_a * grad_y * (sq_y - quartic * squared))
    flux_x = ENERGY_SCALE * (aniso_sq * grad_x + factor_a * grad_x * (sq_x - quartic * squared))
    divergence = 0.5 * (flux_z[2:, 1:-1, 1:-1] - flux_z[:-2, 1:-1, 1:-1])
    divergence = divergence + 0.5 * (flux_y[1:-1, 2:, 1:-1] - flux_y[1:-1, :-2, 1:-1])
    divergence = divergence + 0.5 * (flux_x[1:-1, 1:-1, 2:] - flux_x[1:-1, 1:-1, :-2])
    phase_now = phase_wide[2:-2, 2:-2]
    temp_now = temp_wide[2:-2, 2:-2]
    driving = DRIVE_SCALE / jnp.pi * jnp.arctan(DRIVE_SHARP * (MELT_POINT - temp_now))
    growth = kinetic_rate_field * (
        divergence + phase_now * (1.0 - phase_now) * (phase_now - 0.5 + driving)
    )
    new_phase = phase_now + TIME_STEP * growth
    temp_x = jnp.pad(temp_now, ((0, 0), (0, 0), (1, 1)))
    laplacian = (
        temp_wide[3:-1, 2:-2]
        + temp_wide[1:-3, 2:-2]
        + temp_wide[2:-2, 3:-1]
        + temp_wide[2:-2, 1:-3]
    )
    laplacian = laplacian + temp_x[:, :, 2:] + temp_x[:, :, :-2] - 6.0 * temp_now
    new_temp = temp_now + TIME_STEP * laplacian + LATENT_HEAT * (new_phase - phase_now)
    return (new_phase, new_temp)


def fold_rims(contributions, width, sides):
    for axis, dim in sides:
        size = contributions.shape[dim]
        lower_rim = lax.slice_in_dim(contributions, 0, width, axis=dim)
        upper_rim = lax.slice_in_dim(contributions, size - width, size, axis=dim)
        middle = lax.slice_in_dim(contributions, width, size - width, axis=dim)
        inner = size - 2 * width
        lower_rim, upper_rim = lax.optimization_barrier((lower_rim, upper_rim))
        from_above = from_behind(lower_rim, axis, -1)
        from_below = from_behind(upper_rim, axis, 1)
        contributions = jnp.concatenate(
            (
                lax.slice_in_dim(middle, 0, width, axis=dim) + from_below,
                lax.slice_in_dim(middle, width, inner - width, axis=dim),
                lax.slice_in_dim(middle, inner - width, inner, axis=dim) + from_above,
            ),
            axis=dim,
        )
    return contributions


def inside_grid(cells, margin):
    nz, ny = cells.shape[0] - 2 * margin, cells.shape[1] - 2 * margin
    z = lax.axis_index("gz") * nz - margin + lax.broadcasted_iota(jnp.int32, cells.shape, 0)
    y = lax.axis_index("gy") * ny - margin + lax.broadcasted_iota(jnp.int32, cells.shape, 1)
    total_z = nz * lax.axis_size("gz")
    total_y = ny * lax.axis_size("gy")
    return (z >= 0) & (z < total_z) & (y >= 0) & (y < total_y)


def body(
    saved_order_parameter,
    saved_heat_level,
    kinetic_rate_field,
    order_parameter_adjoint_seed,
    heat_level_adjoint_seed,
):
    state = packed_z_halo(
        jnp.stack((saved_order_parameter, saved_heat_level, kinetic_rate_field)), (4, 3, 2)
    )
    state = extended(state, (("gy", 2),), 4)
    phase_wide, temp_wide, rate_wide = state[0], state[1], state[2]
    succeeding_order_parameter, succeeding_heat_level = advance_solver_step(
        phase_wide, temp_wide, rate_wide[2:-2, 2:-2]
    )
    valid = inside_grid(succeeding_order_parameter, 2)
    succeeding_order_parameter = jnp.where(valid, succeeding_order_parameter, 0.0)
    succeeding_heat_level = jnp.where(valid, succeeding_heat_level, 0.0)
    discarded_result, sensitivity_latest = jax.vjp(
        advance_solver_step,
        succeeding_order_parameter,
        succeeding_heat_level,
        rate_wide[4:-4, 4:-4],
    )
    halfway_order_parameter, halfway_heat_level, latest_kinetic_rate = sensitivity_latest(
        (order_parameter_adjoint_seed, heat_level_adjoint_seed)
    )
    halfway_order_parameter = jnp.where(valid, halfway_order_parameter, 0.0)
    halfway_heat_level = jnp.where(valid, halfway_heat_level, 0.0)
    discarded_result, prior_backward_sweep = jax.vjp(
        advance_solver_step, phase_wide, temp_wide, rate_wide[2:-2, 2:-2]
    )
    sensitivity_order_parameter, sensitivity_heat_level, early_mob = prior_backward_sweep(
        (halfway_order_parameter, halfway_heat_level)
    )
    early_mob = jnp.pad(early_mob, ((2, 2), (2, 2), (0, 0)))
    folded = fold_rims(
        jnp.stack((sensitivity_order_parameter, sensitivity_heat_level, early_mob)),
        4,
        (("gy", 2),),
    )
    folded = packed_z_fold(folded, (4, 3, 2))
    return (folded[0], folded[1], latest_kinetic_rate + folded[2])


def solution(mesh):
    return jax.shard_map(
        body,
        mesh=mesh,
        in_specs=(
            P("gz", "gy", None),
            P("gz", "gy", None),
            P("gz", "gy", None),
            P("gz", "gy", None),
            P("gz", "gy", None),
        ),
        out_specs=(P("gz", "gy", None), P("gz", "gy", None), P("gz", "gy", None)),
        check_vma=False,
    )
```

```python
import jax
import jax.numpy as jnp
from jax import lax
from jax.sharding import PartitionSpec as P

TIME_STEP = 0.15
ENERGY_SCALE = 0.5
ANISOTROPY = 0.05
GRAD_FLOOR = 0.01
LATENT_HEAT = 1.8
DRIVE_SCALE = 0.9
DRIVE_SHARP = 10.0
MELT_POINT = 1.0


def from_behind(block, axis, distance):
    devices = range(lax.axis_size(axis))
    route = [(i - distance, i) for i in devices if i - distance in devices]
    return lax.ppermute(block, axis, route)


def extended(cells, sides, width):
    for axis, dim in sides:
        count = lax.axis_size(axis)
        ends = count - 1
        head = lax.slice_in_dim(cells, 0, width, axis=dim)
        tail = lax.slice_in_dim(cells, cells.shape[dim] - width, cells.shape[dim], axis=dim)
        cells = jnp.concatenate(
            [
                lax.ppermute(tail, axis, [(i, (i + 1) % count) for i in range(ends)]),
                cells,
                lax.ppermute(head, axis, [((i + 1) % count, i) for i in range(ends)]),
            ],
            axis=dim,
        )
    return cells


def packed_z_halo(fields, widths):
    width, size = max(widths), fields[0].shape[0]
    tails = jnp.concatenate([f[size - w :] for f, w in zip(fields, widths)], 0)
    heads = jnp.concatenate([f[:w] for f, w in zip(fields, widths)], 0)
    cells = jnp.stack(fields)
    from_below = from_behind(tails, "gz", 1)
    from_above = from_behind(heads, "gz", -1)
    cuts = [sum(widths[:i]) for i in range(len(widths) + 1)]
    below = jnp.stack(
        [
            jnp.pad(from_below[cuts[i] : cuts[i + 1]], ((width - w, 0), (0, 0), (0, 0)))
            for i, w in enumerate(widths)
        ]
    )
    above = jnp.stack(
        [
            jnp.pad(from_above[cuts[i] : cuts[i + 1]], ((0, width - w), (0, 0), (0, 0)))
            for i, w in enumerate(widths)
        ]
    )
    return jnp.concatenate((below, cells, above), axis=1)


def packed_z_fold(contributions, widths):
    width, size = max(widths), contributions.shape[1]
    lower = jnp.concatenate(
        [contributions[i, width - w : width] for i, w in enumerate(widths)], 0
    )
    upper = jnp.concatenate(
        [contributions[i, size - width : size - width + w] for i, w in enumerate(widths)], 0
    )
    lower, upper = lax.optimization_barrier((lower, upper))
    from_above = from_behind(lower, "gz", -1)
    from_below = from_behind(upper, "gz", 1)
    cuts = [sum(widths[:i]) for i in range(len(widths) + 1)]
    below = jnp.stack(
        [
            jnp.pad(from_below[cuts[i] : cuts[i + 1]], ((0, width - w), (0, 0), (0, 0)))
            for i, w in enumerate(widths)
        ]
    )
    above = jnp.stack(
        [
            jnp.pad(from_above[cuts[i] : cuts[i + 1]], ((width - w, 0), (0, 0), (0, 0)))
            for i, w in enumerate(widths)
        ]
    )
    middle = contributions[:, width : size - width]
    inner = size - 2 * width
    return jnp.concatenate(
        (
            middle[:, :width] + below,
            middle[:, width : inner - width],
            middle[:, inner - width :] + above,
        ),
        axis=1,
    )


def advance_solver_step(phase_wide, temp_wide, kinetic_rate_field):
    padded = jnp.pad(phase_wide, ((0, 0), (0, 0), (2, 2)))
    grad_z = 0.5 * (padded[2:, 1:-1, 1:-1] - padded[:-2, 1:-1, 1:-1])
    grad_y = 0.5 * (padded[1:-1, 2:, 1:-1] - padded[1:-1, :-2, 1:-1])
    grad_x = 0.5 * (padded[1:-1, 1:-1, 2:] - padded[1:-1, 1:-1, :-2])
    sq_z = grad_z * grad_z
    sq_y = grad_y * grad_y
    sq_x = grad_x * grad_x
    squared = sq_z + sq_y + sq_x + GRAD_FLOOR
    quartic = (sq_z * sq_z + sq_y * sq_y + sq_x * sq_x) / (squared * squared)
    anisotropy = 1.0 + ANISOTROPY * (4.0 * quartic - 3.0)
    aniso_sq = anisotropy * anisotropy
    factor_a = 16.0 * ANISOTROPY * anisotropy / squared
    flux_z = ENERGY_SCALE * (aniso_sq * grad_z + factor_a * grad_z * (sq_z - quartic * squared))
    flux_y = ENERGY_SCALE * (aniso_sq * grad_y + factor_a * grad_y * (sq_y - quartic * squared))
    flux_x = ENERGY_SCALE * (aniso_sq * grad_x + factor_a * grad_x * (sq_x - quartic * squared))
    divergence = 0.5 * (flux_z[2:, 1:-1, 1:-1] - flux_z[:-2, 1:-1, 1:-1])
    divergence = divergence + 0.5 * (flux_y[1:-1, 2:, 1:-1] - flux_y[1:-1, :-2, 1:-1])
    divergence = divergence + 0.5 * (flux_x[1:-1, 1:-1, 2:] - flux_x[1:-1, 1:-1, :-2])
    phase_now = phase_wide[2:-2, 2:-2]
    temp_now = temp_wide[2:-2, 2:-2]
    driving = DRIVE_SCALE / jnp.pi * jnp.arctan(DRIVE_SHARP * (MELT_POINT - temp_now))
    growth = kinetic_rate_field * (
        divergence + phase_now * (1.0 - phase_now) * (phase_now - 0.5 + driving)
    )
    new_phase = phase_now + TIME_STEP * growth
    temp_x = jnp.pad(temp_now, ((0, 0), (0, 0), (1, 1)))
    laplacian = (
        temp_wide[3:-1, 2:-2]
        + temp_wide[1:-3, 2:-2]
        + temp_wide[2:-2, 3:-1]
        + temp_wide[2:-2, 1:-3]
    )
    laplacian = laplacian + temp_x[:, :, 2:] + temp_x[:, :, :-2] - 6.0 * temp_now
    new_temp = temp_now + TIME_STEP * laplacian + LATENT_HEAT * (new_phase - phase_now)
    return (new_phase, new_temp)


def fold_rims(contributions, width, sides):
    for axis, dim in sides:
        size = contributions.shape[dim]
        lower_rim = lax.slice_in_dim(contributions, 0, width, axis=dim)
        upper_rim = lax.slice_in_dim(contributions, size - width, size, axis=dim)
        middle = lax.slice_in_dim(contributions, width, size - width, axis=dim)
        inner = size - 2 * width
        lower_rim, upper_rim = lax.optimization_barrier((lower_rim, upper_rim))
        from_above = from_behind(lower_rim, axis, -1)
        from_below = from_behind(upper_rim, axis, 1)
        contributions = jnp.concatenate(
            (
                lax.slice_in_dim(middle, 0, width, axis=dim) + from_below,
                lax.slice_in_dim(middle, width, inner - width, axis=dim),
                lax.slice_in_dim(middle, inner - width, inner, axis=dim) + from_above,
            ),
            axis=dim,
        )
    return contributions


def inside_grid(cells, margin):
    nz, ny = cells.shape[0] - 2 * margin, cells.shape[1] - 2 * margin
    z = lax.axis_index("gz") * nz - margin + lax.broadcasted_iota(jnp.int32, cells.shape, 0)
    y = lax.axis_index("gy") * ny - margin + lax.broadcasted_iota(jnp.int32, cells.shape, 1)
    total_z = nz * lax.axis_size("gz")
    total_y = ny * lax.axis_size("gy")
    return (z >= 0) & (z < total_z) & (y >= 0) & (y < total_y)


def body(
    saved_order_parameter,
    saved_heat_level,
    kinetic_rate_field,
    order_parameter_adjoint_seed,
    heat_level_adjoint_seed,
):
    state = packed_z_halo(
        (saved_order_parameter, saved_heat_level, kinetic_rate_field), (4, 2, 2)
    )
    state = extended(state, (("gy", 2),), 4)
    phase_wide, temp_wide, rate_wide = state[0], state[1], state[2]
    succeeding_order_parameter, succeeding_heat_level = advance_solver_step(
        phase_wide, temp_wide, rate_wide[2:-2, 2:-2]
    )
    valid = inside_grid(succeeding_order_parameter, 2)
    succeeding_order_parameter = jnp.where(valid, succeeding_order_parameter, 0.0)
    succeeding_heat_level = jnp.where(valid, succeeding_heat_level, 0.0)
    discarded_result, sensitivity_latest = jax.vjp(
        advance_solver_step,
        succeeding_order_parameter,
        succeeding_heat_level,
        rate_wide[4:-4, 4:-4],
    )
    halfway_order_parameter, halfway_heat_level, latest_kinetic_rate = sensitivity_latest(
        (order_parameter_adjoint_seed, heat_level_adjoint_seed)
    )
    halfway_order_parameter = jnp.where(valid, halfway_order_parameter, 0.0)
    halfway_heat_level = jnp.where(valid, halfway_heat_level, 0.0)
    discarded_result, prior_backward_sweep = jax.vjp(
        advance_solver_step, phase_wide, temp_wide, rate_wide[2:-2, 2:-2]
    )
    sensitivity_order_parameter, sensitivity_heat_level, early_mob = prior_backward_sweep(
        (halfway_order_parameter, halfway_heat_level)
    )
    early_mob = jnp.pad(early_mob, ((2, 2), (2, 2), (0, 0)))
    folded = fold_rims(
        jnp.stack((sensitivity_order_parameter, sensitivity_heat_level, early_mob)),
        4,
        (("gy", 2),),
    )
    folded = packed_z_fold(folded, (4, 3, 2))
    return (folded[0], folded[1], latest_kinetic_rate + folded[2])


def solution(mesh):
    return jax.shard_map(
        body,
        mesh=mesh,
        in_specs=(
            P("gz", "gy", None),
            P("gz", "gy", None),
            P("gz", "gy", None),
            P("gz", "gy", None),
            P("gz", "gy", None),
        ),
        out_specs=(P("gz", "gy", None), P("gz", "gy", None), P("gz", "gy", None)),
        check_vma=False,
    )
```

```python
import jax
import jax.numpy as jnp
from jax import lax
from jax.sharding import PartitionSpec as P

TIME_STEP = 0.15
ENERGY_SCALE = 0.5
ANISOTROPY = 0.05
GRAD_FLOOR = 0.01
LATENT_HEAT = 1.8
DRIVE_SCALE = 0.9
DRIVE_SHARP = 10.0
MELT_POINT = 1.0


def from_behind(block, axis, distance):
    devices = range(lax.axis_size(axis))
    route = [(i - distance, i) for i in devices if i - distance in devices]
    return lax.ppermute(block, axis, route)


def extended(cells, sides, width):
    for axis, dim in sides:
        count = lax.axis_size(axis)
        ends = count - 1
        head = lax.slice_in_dim(cells, 0, width, axis=dim)
        tail = lax.slice_in_dim(cells, cells.shape[dim] - width, cells.shape[dim], axis=dim)
        cells = jnp.concatenate(
            [
                lax.ppermute(tail, axis, [(i, (i + 1) % count) for i in range(ends)]),
                cells,
                lax.ppermute(head, axis, [((i + 1) % count, i) for i in range(ends)]),
            ],
            axis=dim,
        )
    return cells


def packed_z_halo(fields, widths):
    width, size = max(widths), fields[0].shape[0]
    tails = jnp.concatenate([f[size - w :] for f, w in zip(fields, widths)], 0)
    heads = jnp.concatenate([f[:w] for f, w in zip(fields, widths)], 0)
    cells = jnp.stack(fields)
    from_below = from_behind(tails, "gz", 1)
    from_above = from_behind(heads, "gz", -1)
    cuts = [sum(widths[:i]) for i in range(len(widths) + 1)]
    below = jnp.stack(
        [
            jnp.pad(from_below[cuts[i] : cuts[i + 1]], ((width - w, 0), (0, 0), (0, 0)))
            for i, w in enumerate(widths)
        ]
    )
    above = jnp.stack(
        [
            jnp.pad(from_above[cuts[i] : cuts[i + 1]], ((0, width - w), (0, 0), (0, 0)))
            for i, w in enumerate(widths)
        ]
    )
    return jnp.concatenate((below, cells, above), axis=1)


def packed_z_fold(contributions, widths):
    width, size = max(widths), contributions.shape[1]
    lower = jnp.concatenate(
        [contributions[i, width - w : width] for i, w in enumerate(widths)], 0
    )
    upper = jnp.concatenate(
        [contributions[i, size - width : size - width + w] for i, w in enumerate(widths)], 0
    )
    lower, upper = lax.optimization_barrier((lower, upper))
    from_above = from_behind(lower, "gz", -1)
    from_below = from_behind(upper, "gz", 1)
    cuts = [sum(widths[:i]) for i in range(len(widths) + 1)]
    below = jnp.stack(
        [
            jnp.pad(from_below[cuts[i] : cuts[i + 1]], ((0, width - w), (0, 0), (0, 0)))
            for i, w in enumerate(widths)
        ]
    )
    above = jnp.stack(
        [
            jnp.pad(from_above[cuts[i] : cuts[i + 1]], ((width - w, 0), (0, 0), (0, 0)))
            for i, w in enumerate(widths)
        ]
    )
    middle = contributions[:, width : size - width]
    inner = size - 2 * width
    return jnp.concatenate(
        (
            middle[:, :width] + below,
            middle[:, width : inner - width],
            middle[:, inner - width :] + above,
        ),
        axis=1,
    )


def packed_y_halo(cells):
    depth, rows = cells.shape[1], cells.shape[2]

    def rims(lo, hi, narrow):
        return jnp.concatenate(
            (
                cells[0, :, lo:hi],
                jnp.concatenate(
                    (cells[1, 2 : depth - 2, narrow], cells[2, 2 : depth - 2, narrow]), axis=1
                ),
            ),
            axis=0,
        )

    lower = rims(0, 4, slice(0, 2))
    upper = rims(rows - 4, rows, slice(rows - 2, rows))
    lower, upper = lax.optimization_barrier((lower, upper))
    from_above = from_behind(lower, "gy", -1)
    from_below = from_behind(upper, "gy", 1)

    def unpack(arrived, outer):
        narrow = arrived[depth:]
        spread = ((2, 2), outer, (0, 0))
        return jnp.stack(
            (
                arrived[:depth],
                jnp.pad(narrow[:, :2], spread),
                jnp.pad(narrow[:, 2:], spread),
            )
        )

    return jnp.concatenate(
        (unpack(from_below, (2, 0)), cells, unpack(from_above, (0, 2))), axis=2
    )


def packed_y_fold(contributions):
    depth, rows = contributions.shape[1], contributions.shape[2]

    def rims(lo, hi):
        return jnp.concatenate(
            (
                contributions[0, :, lo:hi],
                contributions[1, 1 : depth - 1, lo:hi],
                contributions[2, 2 : depth - 2, lo:hi],
            ),
            axis=0,
        )

    lower = rims(0, 4)
    upper = rims(rows - 4, rows)
    lower, upper = lax.optimization_barrier((lower, upper))
    from_above = from_behind(lower, "gy", -1)
    from_below = from_behind(upper, "gy", 1)

    def unpack(arrived):
        return jnp.stack(
            (
                arrived[:depth],
                jnp.pad(arrived[depth : 2 * depth - 2], ((1, 1), (0, 0), (0, 0))),
                jnp.pad(arrived[2 * depth - 2 :], ((2, 2), (0, 0), (0, 0))),
            )
        )

    middle = contributions[:, :, 4 : rows - 4]
    return jnp.concatenate(
        (
            middle[:, :, :4] + unpack(from_below),
            middle[:, :, 4:-4],
            middle[:, :, -4:] + unpack(from_above),
        ),
        axis=2,
    )


def advance_solver_step(phase_wide, temp_wide, kinetic_rate_field):
    padded = jnp.pad(phase_wide, ((0, 0), (0, 0), (2, 2)))
    grad_z = 0.5 * (padded[2:, 1:-1, 1:-1] - padded[:-2, 1:-1, 1:-1])
    grad_y = 0.5 * (padded[1:-1, 2:, 1:-1] - padded[1:-1, :-2, 1:-1])
    grad_x = 0.5 * (padded[1:-1, 1:-1, 2:] - padded[1:-1, 1:-1, :-2])
    sq_z = grad_z * grad_z
    sq_y = grad_y * grad_y
    sq_x = grad_x * grad_x
    squared = sq_z + sq_y + sq_x + GRAD_FLOOR
    quartic = (sq_z * sq_z + sq_y * sq_y + sq_x * sq_x) / (squared * squared)
    anisotropy = 1.0 + ANISOTROPY * (4.0 * quartic - 3.0)
    aniso_sq = anisotropy * anisotropy
    factor_a = 16.0 * ANISOTROPY * anisotropy / squared
    flux_z = ENERGY_SCALE * (aniso_sq * grad_z + factor_a * grad_z * (sq_z - quartic * squared))
    flux_y = ENERGY_SCALE * (aniso_sq * grad_y + factor_a * grad_y * (sq_y - quartic * squared))
    flux_x = ENERGY_SCALE * (aniso_sq * grad_x + factor_a * grad_x * (sq_x - quartic * squared))
    divergence = 0.5 * (flux_z[2:, 1:-1, 1:-1] - flux_z[:-2, 1:-1, 1:-1])
    divergence = divergence + 0.5 * (flux_y[1:-1, 2:, 1:-1] - flux_y[1:-1, :-2, 1:-1])
    divergence = divergence + 0.5 * (flux_x[1:-1, 1:-1, 2:] - flux_x[1:-1, 1:-1, :-2])
    phase_now = phase_wide[2:-2, 2:-2]
    temp_now = temp_wide[2:-2, 2:-2]
    driving = DRIVE_SCALE / jnp.pi * jnp.arctan(DRIVE_SHARP * (MELT_POINT - temp_now))
    growth = kinetic_rate_field * (
        divergence + phase_now * (1.0 - phase_now) * (phase_now - 0.5 + driving)
    )
    new_phase = phase_now + TIME_STEP * growth
    temp_x = jnp.pad(temp_now, ((0, 0), (0, 0), (1, 1)))
    laplacian = (
        temp_wide[3:-1, 2:-2]
        + temp_wide[1:-3, 2:-2]
        + temp_wide[2:-2, 3:-1]
        + temp_wide[2:-2, 1:-3]
    )
    laplacian = laplacian + temp_x[:, :, 2:] + temp_x[:, :, :-2] - 6.0 * temp_now
    new_temp = temp_now + TIME_STEP * laplacian + LATENT_HEAT * (new_phase - phase_now)
    return (new_phase, new_temp)


def fold_rims(contributions, width, sides):
    for axis, dim in sides:
        size = contributions.shape[dim]
        lower_rim = lax.slice_in_dim(contributions, 0, width, axis=dim)
        upper_rim = lax.slice_in_dim(contributions, size - width, size, axis=dim)
        middle = lax.slice_in_dim(contributions, width, size - width, axis=dim)
        inner = size - 2 * width
        lower_rim, upper_rim = lax.optimization_barrier((lower_rim, upper_rim))
        from_above = from_behind(lower_rim, axis, -1)
        from_below = from_behind(upper_rim, axis, 1)
        contributions = jnp.concatenate(
            (
                lax.slice_in_dim(middle, 0, width, axis=dim) + from_below,
                lax.slice_in_dim(middle, width, inner - width, axis=dim),
                lax.slice_in_dim(middle, inner - width, inner, axis=dim) + from_above,
            ),
            axis=dim,
        )
    return contributions


def inside_grid(cells, margin):
    nz, ny = cells.shape[0] - 2 * margin, cells.shape[1] - 2 * margin
    z = lax.axis_index("gz") * nz - margin + lax.broadcasted_iota(jnp.int32, cells.shape, 0)
    y = lax.axis_index("gy") * ny - margin + lax.broadcasted_iota(jnp.int32, cells.shape, 1)
    total_z = nz * lax.axis_size("gz")
    total_y = ny * lax.axis_size("gy")
    return (z >= 0) & (z < total_z) & (y >= 0) & (y < total_y)


def body(
    saved_order_parameter,
    saved_heat_level,
    kinetic_rate_field,
    order_parameter_adjoint_seed,
    heat_level_adjoint_seed,
):
    state = packed_z_halo(
        (saved_order_parameter, saved_heat_level, kinetic_rate_field), (4, 2, 2)
    )
    state = packed_y_halo(state)
    phase_wide, temp_wide, rate_wide = state[0], state[1], state[2]
    succeeding_order_parameter, succeeding_heat_level = advance_solver_step(
        phase_wide, temp_wide, rate_wide[2:-2, 2:-2]
    )
    valid = inside_grid(succeeding_order_parameter, 2)
    succeeding_order_parameter = jnp.where(valid, succeeding_order_parameter, 0.0)
    succeeding_heat_level = jnp.where(valid, succeeding_heat_level, 0.0)
    discarded_result, sensitivity_latest = jax.vjp(
        advance_solver_step,
        succeeding_order_parameter,
        succeeding_heat_level,
        rate_wide[4:-4, 4:-4],
    )
    halfway_order_parameter, halfway_heat_level, latest_kinetic_rate = sensitivity_latest(
        (order_parameter_adjoint_seed, heat_level_adjoint_seed)
    )
    halfway_order_parameter = jnp.where(valid, halfway_order_parameter, 0.0)
    halfway_heat_level = jnp.where(valid, halfway_heat_level, 0.0)
    discarded_result, prior_backward_sweep = jax.vjp(
        advance_solver_step, phase_wide, temp_wide, rate_wide[2:-2, 2:-2]
    )
    sensitivity_order_parameter, sensitivity_heat_level, early_mob = prior_backward_sweep(
        (halfway_order_parameter, halfway_heat_level)
    )
    early_mob = jnp.pad(early_mob, ((2, 2), (2, 2), (0, 0)))
    folded = packed_y_fold(
        jnp.stack((sensitivity_order_parameter, sensitivity_heat_level, early_mob))
    )
    folded = packed_z_fold(folded, (4, 3, 2))
    return (folded[0], folded[1], latest_kinetic_rate + folded[2])


def solution(mesh):
    return jax.shard_map(
        body,
        mesh=mesh,
        in_specs=(
            P("gz", "gy", None),
            P("gz", "gy", None),
            P("gz", "gy", None),
            P("gz", "gy", None),
            P("gz", "gy", None),
        ),
        out_specs=(P("gz", "gy", None), P("gz", "gy", None), P("gz", "gy", None)),
        check_vma=False,
    )
```

```python
import jax
import jax.numpy as jnp
from jax import lax
from jax.sharding import PartitionSpec as P

TIME_STEP = 0.15
ENERGY_SCALE = 0.5
ANISOTROPY = 0.05
GRAD_FLOOR = 0.01
LATENT_HEAT = 1.8
DRIVE_SCALE = 0.9
DRIVE_SHARP = 10.0
MELT_POINT = 1.0


def from_behind(block, axis, distance):
    devices = range(lax.axis_size(axis))
    route = [(i - distance, i) for i in devices if i - distance in devices]
    return lax.ppermute(block, axis, route)


def extended(cells, sides, width):
    for axis, dim in sides:
        count = lax.axis_size(axis)
        ends = count - 1
        head = lax.slice_in_dim(cells, 0, width, axis=dim)
        tail = lax.slice_in_dim(cells, cells.shape[dim] - width, cells.shape[dim], axis=dim)
        cells = jnp.concatenate(
            [
                lax.ppermute(tail, axis, [(i, (i + 1) % count) for i in range(ends)]),
                cells,
                lax.ppermute(head, axis, [((i + 1) % count, i) for i in range(ends)]),
            ],
            axis=dim,
        )
    return cells


def packed_z_halo(fields, widths):
    width, size = max(widths), fields[0].shape[0]
    tails = jnp.concatenate([f[size - w :] for f, w in zip(fields, widths)], 0)
    heads = jnp.concatenate([f[:w] for f, w in zip(fields, widths)], 0)
    cells = jnp.stack(fields)
    from_below = from_behind(tails, "gz", 1)
    from_above = from_behind(heads, "gz", -1)
    cuts = [sum(widths[:i]) for i in range(len(widths) + 1)]
    below = jnp.stack(
        [
            jnp.pad(from_below[cuts[i] : cuts[i + 1]], ((width - w, 0), (0, 0), (0, 0)))
            for i, w in enumerate(widths)
        ]
    )
    above = jnp.stack(
        [
            jnp.pad(from_above[cuts[i] : cuts[i + 1]], ((0, width - w), (0, 0), (0, 0)))
            for i, w in enumerate(widths)
        ]
    )
    return jnp.concatenate((below, cells, above), axis=1)


def packed_z_fold(contributions, widths):
    width, size = max(widths), contributions.shape[1]
    lower = jnp.concatenate(
        [contributions[i, width - w : width] for i, w in enumerate(widths)], 0
    )
    upper = jnp.concatenate(
        [contributions[i, size - width : size - width + w] for i, w in enumerate(widths)], 0
    )
    lower, upper = lax.optimization_barrier((lower, upper))
    from_above = from_behind(lower, "gz", -1)
    from_below = from_behind(upper, "gz", 1)
    cuts = [sum(widths[:i]) for i in range(len(widths) + 1)]
    below = jnp.stack(
        [
            jnp.pad(from_below[cuts[i] : cuts[i + 1]], ((0, width - w), (0, 0), (0, 0)))
            for i, w in enumerate(widths)
        ]
    )
    above = jnp.stack(
        [
            jnp.pad(from_above[cuts[i] : cuts[i + 1]], ((width - w, 0), (0, 0), (0, 0)))
            for i, w in enumerate(widths)
        ]
    )
    middle = contributions[:, width : size - width]
    inner = size - 2 * width
    return jnp.concatenate(
        (
            middle[:, :width] + below,
            middle[:, width : inner - width],
            middle[:, inner - width :] + above,
        ),
        axis=1,
    )


def packed_y_halo(cells):
    depth, rows = cells.shape[1], cells.shape[2]

    def rims(lo, hi, narrow):
        return jnp.concatenate(
            (
                cells[0, :, lo:hi],
                jnp.concatenate(
                    (cells[1, 2 : depth - 2, narrow], cells[2, 2 : depth - 2, narrow]), axis=1
                ),
            ),
            axis=0,
        )

    lower = rims(0, 4, slice(0, 2))
    upper = rims(rows - 4, rows, slice(rows - 2, rows))
    lower, upper = lax.optimization_barrier((lower, upper))
    from_above = from_behind(lower, "gy", -1)
    from_below = from_behind(upper, "gy", 1)

    def unpack(arrived, outer):
        narrow = arrived[depth:]
        spread = ((2, 2), outer, (0, 0))
        return jnp.stack(
            (
                arrived[:depth],
                jnp.pad(narrow[:, :2], spread),
                jnp.pad(narrow[:, 2:], spread),
            )
        )

    return jnp.concatenate(
        (unpack(from_below, (2, 0)), cells, unpack(from_above, (0, 2))), axis=2
    )


def packed_y_fold(contributions):
    depth, rows = contributions.shape[1], contributions.shape[2]

    lanes = contributions.shape[3]

    def rims(lo, hi, narrow):
        return jnp.concatenate(
            (
                contributions[0, :, lo:hi],
                contributions[1, 1 : depth - 1, lo:hi],
                contributions[2, 2 : depth - 2, narrow].reshape(-1, 4, lanes),
            ),
            axis=0,
        )

    lower = rims(0, 4, slice(2, 4))
    upper = rims(rows - 4, rows, slice(rows - 4, rows - 2))
    lower, upper = lax.optimization_barrier((lower, upper))
    from_above = from_behind(lower, "gy", -1)
    from_below = from_behind(upper, "gy", 1)

    def unpack(arrived, outer):
        narrow = arrived[2 * depth - 2 :].reshape(depth - 4, 2, lanes)
        return jnp.stack(
            (
                arrived[:depth],
                jnp.pad(arrived[depth : 2 * depth - 2], ((1, 1), (0, 0), (0, 0))),
                jnp.pad(narrow, ((2, 2), outer, (0, 0))),
            )
        )

    middle = contributions[:, :, 4 : rows - 4]
    return jnp.concatenate(
        (
            middle[:, :, :4] + unpack(from_below, (0, 2)),
            middle[:, :, 4:-4],
            middle[:, :, -4:] + unpack(from_above, (2, 0)),
        ),
        axis=2,
    )


def advance_solver_step(phase_wide, temp_wide, kinetic_rate_field):
    padded = jnp.pad(phase_wide, ((0, 0), (0, 0), (2, 2)))
    grad_z = 0.5 * (padded[2:, 1:-1, 1:-1] - padded[:-2, 1:-1, 1:-1])
    grad_y = 0.5 * (padded[1:-1, 2:, 1:-1] - padded[1:-1, :-2, 1:-1])
    grad_x = 0.5 * (padded[1:-1, 1:-1, 2:] - padded[1:-1, 1:-1, :-2])
    sq_z = grad_z * grad_z
    sq_y = grad_y * grad_y
    sq_x = grad_x * grad_x
    squared = sq_z + sq_y + sq_x + GRAD_FLOOR
    quartic = (sq_z * sq_z + sq_y * sq_y + sq_x * sq_x) / (squared * squared)
    anisotropy = 1.0 + ANISOTROPY * (4.0 * quartic - 3.0)
    aniso_sq = anisotropy * anisotropy
    factor_a = 16.0 * ANISOTROPY * anisotropy / squared
    flux_z = ENERGY_SCALE * (aniso_sq * grad_z + factor_a * grad_z * (sq_z - quartic * squared))
    flux_y = ENERGY_SCALE * (aniso_sq * grad_y + factor_a * grad_y * (sq_y - quartic * squared))
    flux_x = ENERGY_SCALE * (aniso_sq * grad_x + factor_a * grad_x * (sq_x - quartic * squared))
    divergence = 0.5 * (flux_z[2:, 1:-1, 1:-1] - flux_z[:-2, 1:-1, 1:-1])
    divergence = divergence + 0.5 * (flux_y[1:-1, 2:, 1:-1] - flux_y[1:-1, :-2, 1:-1])
    divergence = divergence + 0.5 * (flux_x[1:-1, 1:-1, 2:] - flux_x[1:-1, 1:-1, :-2])
    phase_now = phase_wide[2:-2, 2:-2]
    temp_now = temp_wide[2:-2, 2:-2]
    driving = DRIVE_SCALE / jnp.pi * jnp.arctan(DRIVE_SHARP * (MELT_POINT - temp_now))
    growth = kinetic_rate_field * (
        divergence + phase_now * (1.0 - phase_now) * (phase_now - 0.5 + driving)
    )
    new_phase = phase_now + TIME_STEP * growth
    temp_x = jnp.pad(temp_now, ((0, 0), (0, 0), (1, 1)))
    laplacian = (
        temp_wide[3:-1, 2:-2]
        + temp_wide[1:-3, 2:-2]
        + temp_wide[2:-2, 3:-1]
        + temp_wide[2:-2, 1:-3]
    )
    laplacian = laplacian + temp_x[:, :, 2:] + temp_x[:, :, :-2] - 6.0 * temp_now
    new_temp = temp_now + TIME_STEP * laplacian + LATENT_HEAT * (new_phase - phase_now)
    return (new_phase, new_temp)


def fold_rims(contributions, width, sides):
    for axis, dim in sides:
        size = contributions.shape[dim]
        lower_rim = lax.slice_in_dim(contributions, 0, width, axis=dim)
        upper_rim = lax.slice_in_dim(contributions, size - width, size, axis=dim)
        middle = lax.slice_in_dim(contributions, width, size - width, axis=dim)
        inner = size - 2 * width
        lower_rim, upper_rim = lax.optimization_barrier((lower_rim, upper_rim))
        from_above = from_behind(lower_rim, axis, -1)
        from_below = from_behind(upper_rim, axis, 1)
        contributions = jnp.concatenate(
            (
                lax.slice_in_dim(middle, 0, width, axis=dim) + from_below,
                lax.slice_in_dim(middle, width, inner - width, axis=dim),
                lax.slice_in_dim(middle, inner - width, inner, axis=dim) + from_above,
            ),
            axis=dim,
        )
    return contributions


def inside_grid(cells, margin):
    nz, ny = cells.shape[0] - 2 * margin, cells.shape[1] - 2 * margin
    z = lax.axis_index("gz") * nz - margin + lax.broadcasted_iota(jnp.int32, cells.shape, 0)
    y = lax.axis_index("gy") * ny - margin + lax.broadcasted_iota(jnp.int32, cells.shape, 1)
    total_z = nz * lax.axis_size("gz")
    total_y = ny * lax.axis_size("gy")
    return (z >= 0) & (z < total_z) & (y >= 0) & (y < total_y)


def body(
    saved_order_parameter,
    saved_heat_level,
    kinetic_rate_field,
    order_parameter_adjoint_seed,
    heat_level_adjoint_seed,
):
    state = packed_z_halo(
        (saved_order_parameter, saved_heat_level, kinetic_rate_field), (4, 2, 2)
    )
    state = packed_y_halo(state)
    phase_wide, temp_wide, rate_wide = state[0], state[1], state[2]
    succeeding_order_parameter, succeeding_heat_level = advance_solver_step(
        phase_wide, temp_wide, rate_wide[2:-2, 2:-2]
    )
    valid = inside_grid(succeeding_order_parameter, 2)
    succeeding_order_parameter = jnp.where(valid, succeeding_order_parameter, 0.0)
    succeeding_heat_level = jnp.where(valid, succeeding_heat_level, 0.0)
    discarded_result, sensitivity_latest = jax.vjp(
        advance_solver_step,
        succeeding_order_parameter,
        succeeding_heat_level,
        rate_wide[4:-4, 4:-4],
    )
    halfway_order_parameter, halfway_heat_level, latest_kinetic_rate = sensitivity_latest(
        (order_parameter_adjoint_seed, heat_level_adjoint_seed)
    )
    halfway_order_parameter = jnp.where(valid, halfway_order_parameter, 0.0)
    halfway_heat_level = jnp.where(valid, halfway_heat_level, 0.0)
    discarded_result, prior_backward_sweep = jax.vjp(
        advance_solver_step, phase_wide, temp_wide, rate_wide[2:-2, 2:-2]
    )
    sensitivity_order_parameter, sensitivity_heat_level, early_mob = prior_backward_sweep(
        (halfway_order_parameter, halfway_heat_level)
    )
    early_mob = jnp.pad(early_mob, ((2, 2), (2, 2), (0, 0)))
    folded = packed_y_fold(
        jnp.stack((sensitivity_order_parameter, sensitivity_heat_level, early_mob))
    )
    folded = packed_z_fold(folded, (4, 3, 2))
    return (folded[0], folded[1], latest_kinetic_rate + folded[2])


def solution(mesh):
    return jax.shard_map(
        body,
        mesh=mesh,
        in_specs=(
            P("gz", "gy", None),
            P("gz", "gy", None),
            P("gz", "gy", None),
            P("gz", "gy", None),
            P("gz", "gy", None),
        ),
        out_specs=(P("gz", "gy", None), P("gz", "gy", None), P("gz", "gy", None)),
        check_vma=False,
    )
```

```python
import jax
import jax.numpy as jnp
from jax import lax
from jax.sharding import PartitionSpec as P

TIME_STEP = 0.15
ENERGY_SCALE = 0.5
ANISOTROPY = 0.05
GRAD_FLOOR = 0.01
LATENT_HEAT = 1.8
DRIVE_SCALE = 0.9
DRIVE_SHARP = 10.0
MELT_POINT = 1.0


def from_behind(block, axis, distance):
    devices = range(lax.axis_size(axis))
    route = [(i - distance, i) for i in devices if i - distance in devices]
    return lax.ppermute(block, axis, route)


def extended(cells, sides, width):
    for axis, dim in sides:
        count = lax.axis_size(axis)
        ends = count - 1
        head = lax.slice_in_dim(cells, 0, width, axis=dim)
        tail = lax.slice_in_dim(cells, cells.shape[dim] - width, cells.shape[dim], axis=dim)
        cells = jnp.concatenate(
            [
                lax.ppermute(tail, axis, [(i, (i + 1) % count) for i in range(ends)]),
                cells,
                lax.ppermute(head, axis, [((i + 1) % count, i) for i in range(ends)]),
            ],
            axis=dim,
        )
    return cells


def packed_z_halo(fields, widths):
    width, size = max(widths), fields[0].shape[0]
    tails = jnp.concatenate([f[size - w :] for f, w in zip(fields, widths)], 0)
    heads = jnp.concatenate([f[:w] for f, w in zip(fields, widths)], 0)
    cells = jnp.stack(fields)
    from_below = from_behind(tails, "gz", 1)
    from_above = from_behind(heads, "gz", -1)
    cuts = [sum(widths[:i]) for i in range(len(widths) + 1)]
    below = jnp.stack(
        [
            jnp.pad(from_below[cuts[i] : cuts[i + 1]], ((width - w, 0), (0, 0), (0, 0)))
            for i, w in enumerate(widths)
        ]
    )
    above = jnp.stack(
        [
            jnp.pad(from_above[cuts[i] : cuts[i + 1]], ((0, width - w), (0, 0), (0, 0)))
            for i, w in enumerate(widths)
        ]
    )
    return jnp.concatenate((below, cells, above), axis=1)


def packed_z_fold(contributions, widths):
    width, size = max(widths), contributions.shape[1]
    lower = jnp.concatenate(
        [contributions[i, width - w : width] for i, w in enumerate(widths)], 0
    )
    upper = jnp.concatenate(
        [contributions[i, size - width : size - width + w] for i, w in enumerate(widths)], 0
    )
    lower, upper = lax.optimization_barrier((lower, upper))
    from_above = from_behind(lower, "gz", -1)
    from_below = from_behind(upper, "gz", 1)
    cuts = [sum(widths[:i]) for i in range(len(widths) + 1)]
    below = jnp.stack(
        [
            jnp.pad(from_below[cuts[i] : cuts[i + 1]], ((0, width - w), (0, 0), (0, 0)))
            for i, w in enumerate(widths)
        ]
    )
    above = jnp.stack(
        [
            jnp.pad(from_above[cuts[i] : cuts[i + 1]], ((width - w, 0), (0, 0), (0, 0)))
            for i, w in enumerate(widths)
        ]
    )
    middle = contributions[:, width : size - width]
    inner = size - 2 * width
    return jnp.concatenate(
        (
            middle[:, :width] + below,
            middle[:, width : inner - width],
            middle[:, inner - width :] + above,
        ),
        axis=1,
    )


def packed_y_halo(cells):
    depth, rows = cells.shape[1], cells.shape[2]

    def rims(lo, hi, narrow):
        return jnp.concatenate(
            (
                cells[0, :, lo:hi],
                jnp.concatenate(
                    (cells[1, 2 : depth - 2, narrow], cells[2, 2 : depth - 2, narrow]), axis=1
                ),
            ),
            axis=0,
        )

    lower = rims(0, 4, slice(0, 2))
    upper = rims(rows - 4, rows, slice(rows - 2, rows))
    lower, upper = lax.optimization_barrier((lower, upper))
    from_above = from_behind(lower, "gy", -1)
    from_below = from_behind(upper, "gy", 1)

    def unpack(arrived, outer):
        narrow = arrived[depth:]
        spread = ((2, 2), outer, (0, 0))
        return jnp.stack(
            (
                arrived[:depth],
                jnp.pad(narrow[:, :2], spread),
                jnp.pad(narrow[:, 2:], spread),
            )
        )

    return jnp.concatenate(
        (unpack(from_below, (2, 0)), cells, unpack(from_above, (0, 2))), axis=2
    )


def packed_y_fold(contributions):
    depth, rows = contributions.shape[1], contributions.shape[2]

    def rims(lo, hi):
        return jnp.concatenate(
            (
                contributions[0, :, lo:hi],
                contributions[1, 1 : depth - 1, lo:hi],
                contributions[2, 2 : depth - 2, lo:hi],
            ),
            axis=0,
        )

    lower = rims(0, 4)
    upper = rims(rows - 4, rows)
    lower, upper = lax.optimization_barrier((lower, upper))
    from_above = from_behind(lower, "gy", -1)
    from_below = from_behind(upper, "gy", 1)

    def unpack(arrived):
        return jnp.stack(
            (
                arrived[:depth],
                jnp.pad(arrived[depth : 2 * depth - 2], ((1, 1), (0, 0), (0, 0))),
                jnp.pad(arrived[2 * depth - 2 :], ((2, 2), (0, 0), (0, 0))),
            )
        )

    middle = contributions[:, :, 4 : rows - 4]
    return jnp.concatenate(
        (
            middle[:, :, :4] + unpack(from_below),
            middle[:, :, 4:-4],
            middle[:, :, -4:] + unpack(from_above),
        ),
        axis=2,
    )


def advance_solver_step(phase_wide, temp_wide, kinetic_rate_field):
    padded = jnp.pad(phase_wide, ((0, 0), (0, 0), (2, 2)))
    grad_z = 0.5 * (padded[2:, 1:-1, 1:-1] - padded[:-2, 1:-1, 1:-1])
    grad_y = 0.5 * (padded[1:-1, 2:, 1:-1] - padded[1:-1, :-2, 1:-1])
    grad_x = 0.5 * (padded[1:-1, 1:-1, 2:] - padded[1:-1, 1:-1, :-2])
    sq_z = grad_z * grad_z
    sq_y = grad_y * grad_y
    sq_x = grad_x * grad_x
    squared = sq_z + sq_y + sq_x + GRAD_FLOOR
    inverse = 1.0 / squared
    quartic_times_squared = (sq_z * sq_z + sq_y * sq_y + sq_x * sq_x) * inverse
    quartic = quartic_times_squared * inverse
    anisotropy = 1.0 + ANISOTROPY * (4.0 * quartic - 3.0)
    aniso_sq = anisotropy * anisotropy
    factor_a = 16.0 * ANISOTROPY * anisotropy * inverse
    flux_z = ENERGY_SCALE * (aniso_sq * grad_z + factor_a * grad_z * (sq_z - quartic_times_squared))
    flux_y = ENERGY_SCALE * (aniso_sq * grad_y + factor_a * grad_y * (sq_y - quartic_times_squared))
    flux_x = ENERGY_SCALE * (aniso_sq * grad_x + factor_a * grad_x * (sq_x - quartic_times_squared))
    divergence = 0.5 * (flux_z[2:, 1:-1, 1:-1] - flux_z[:-2, 1:-1, 1:-1])
    divergence = divergence + 0.5 * (flux_y[1:-1, 2:, 1:-1] - flux_y[1:-1, :-2, 1:-1])
    divergence = divergence + 0.5 * (flux_x[1:-1, 1:-1, 2:] - flux_x[1:-1, 1:-1, :-2])
    phase_now = phase_wide[2:-2, 2:-2]
    temp_now = temp_wide[2:-2, 2:-2]
    driving = DRIVE_SCALE / jnp.pi * jnp.arctan(DRIVE_SHARP * (MELT_POINT - temp_now))
    growth = kinetic_rate_field * (
        divergence + phase_now * (1.0 - phase_now) * (phase_now - 0.5 + driving)
    )
    new_phase = phase_now + TIME_STEP * growth
    temp_x = jnp.pad(temp_now, ((0, 0), (0, 0), (1, 1)))
    laplacian = (
        temp_wide[3:-1, 2:-2]
        + temp_wide[1:-3, 2:-2]
        + temp_wide[2:-2, 3:-1]
        + temp_wide[2:-2, 1:-3]
    )
    laplacian = laplacian + temp_x[:, :, 2:] + temp_x[:, :, :-2] - 6.0 * temp_now
    new_temp = temp_now + TIME_STEP * laplacian + LATENT_HEAT * (new_phase - phase_now)
    return (new_phase, new_temp)


def fold_rims(contributions, width, sides):
    for axis, dim in sides:
        size = contributions.shape[dim]
        lower_rim = lax.slice_in_dim(contributions, 0, width, axis=dim)
        upper_rim = lax.slice_in_dim(contributions, size - width, size, axis=dim)
        middle = lax.slice_in_dim(contributions, width, size - width, axis=dim)
        inner = size - 2 * width
        lower_rim, upper_rim = lax.optimization_barrier((lower_rim, upper_rim))
        from_above = from_behind(lower_rim, axis, -1)
        from_below = from_behind(upper_rim, axis, 1)
        contributions = jnp.concatenate(
            (
                lax.slice_in_dim(middle, 0, width, axis=dim) + from_below,
                lax.slice_in_dim(middle, width, inner - width, axis=dim),
                lax.slice_in_dim(middle, inner - width, inner, axis=dim) + from_above,
            ),
            axis=dim,
        )
    return contributions


def inside_grid(cells, margin):
    nz, ny = cells.shape[0] - 2 * margin, cells.shape[1] - 2 * margin
    z = lax.axis_index("gz") * nz - margin + lax.broadcasted_iota(jnp.int32, cells.shape, 0)
    y = lax.axis_index("gy") * ny - margin + lax.broadcasted_iota(jnp.int32, cells.shape, 1)
    total_z = nz * lax.axis_size("gz")
    total_y = ny * lax.axis_size("gy")
    return (z >= 0) & (z < total_z) & (y >= 0) & (y < total_y)


def body(
    saved_order_parameter,
    saved_heat_level,
    kinetic_rate_field,
    order_parameter_adjoint_seed,
    heat_level_adjoint_seed,
):
    state = packed_z_halo(
        (saved_order_parameter, saved_heat_level, kinetic_rate_field), (4, 2, 2)
    )
    state = packed_y_halo(state)
    phase_wide, temp_wide, rate_wide = state[0], state[1], state[2]
    succeeding_order_parameter, succeeding_heat_level = advance_solver_step(
        phase_wide, temp_wide, rate_wide[2:-2, 2:-2]
    )
    valid = inside_grid(succeeding_order_parameter, 2)
    succeeding_order_parameter = jnp.where(valid, succeeding_order_parameter, 0.0)
    succeeding_heat_level = jnp.where(valid, succeeding_heat_level, 0.0)
    discarded_result, sensitivity_latest = jax.vjp(
        advance_solver_step,
        succeeding_order_parameter,
        succeeding_heat_level,
        rate_wide[4:-4, 4:-4],
    )
    halfway_order_parameter, halfway_heat_level, latest_kinetic_rate = sensitivity_latest(
        (order_parameter_adjoint_seed, heat_level_adjoint_seed)
    )
    halfway_order_parameter = jnp.where(valid, halfway_order_parameter, 0.0)
    halfway_heat_level = jnp.where(valid, halfway_heat_level, 0.0)
    discarded_result, prior_backward_sweep = jax.vjp(
        advance_solver_step, phase_wide, temp_wide, rate_wide[2:-2, 2:-2]
    )
    sensitivity_order_parameter, sensitivity_heat_level, early_mob = prior_backward_sweep(
        (halfway_order_parameter, halfway_heat_level)
    )
    early_mob = jnp.pad(early_mob, ((2, 2), (2, 2), (0, 0)))
    folded = packed_y_fold(
        jnp.stack((sensitivity_order_parameter, sensitivity_heat_level, early_mob))
    )
    folded = packed_z_fold(folded, (4, 3, 2))
    return (folded[0], folded[1], latest_kinetic_rate + folded[2])


def solution(mesh):
    return jax.shard_map(
        body,
        mesh=mesh,
        in_specs=(
            P("gz", "gy", None),
            P("gz", "gy", None),
            P("gz", "gy", None),
            P("gz", "gy", None),
            P("gz", "gy", None),
        ),
        out_specs=(P("gz", "gy", None), P("gz", "gy", None), P("gz", "gy", None)),
        check_vma=False,
    )
```

```python
import jax
import jax.numpy as jnp
from jax import lax
from jax.sharding import PartitionSpec as P

TIME_STEP = 0.15
ENERGY_SCALE = 0.5
ANISOTROPY = 0.05
GRAD_FLOOR = 0.01
LATENT_HEAT = 1.8
DRIVE_SCALE = 0.9
DRIVE_SHARP = 10.0
MELT_POINT = 1.0


def from_behind(block, axis, distance):
    devices = range(lax.axis_size(axis))
    route = [(i - distance, i) for i in devices if i - distance in devices]
    return lax.ppermute(block, axis, route)


def extended(cells, sides, width):
    for axis, dim in sides:
        count = lax.axis_size(axis)
        ends = count - 1
        head = lax.slice_in_dim(cells, 0, width, axis=dim)
        tail = lax.slice_in_dim(cells, cells.shape[dim] - width, cells.shape[dim], axis=dim)
        cells = jnp.concatenate(
            [
                lax.ppermute(tail, axis, [(i, (i + 1) % count) for i in range(ends)]),
                cells,
                lax.ppermute(head, axis, [((i + 1) % count, i) for i in range(ends)]),
            ],
            axis=dim,
        )
    return cells


def packed_z_halo(fields, widths):
    width, size = max(widths), fields[0].shape[0]
    tails = jnp.concatenate([f[size - w :] for f, w in zip(fields, widths)], 0)
    heads = jnp.concatenate([f[:w] for f, w in zip(fields, widths)], 0)
    cells = jnp.stack(fields)
    from_below = from_behind(tails, "gz", 1)
    from_above = from_behind(heads, "gz", -1)
    cuts = [sum(widths[:i]) for i in range(len(widths) + 1)]
    below = jnp.stack(
        [
            jnp.pad(from_below[cuts[i] : cuts[i + 1]], ((width - w, 0), (0, 0), (0, 0)))
            for i, w in enumerate(widths)
        ]
    )
    above = jnp.stack(
        [
            jnp.pad(from_above[cuts[i] : cuts[i + 1]], ((0, width - w), (0, 0), (0, 0)))
            for i, w in enumerate(widths)
        ]
    )
    return jnp.concatenate((below, cells, above), axis=1)


def packed_z_fold(contributions, widths):
    width, size = max(widths), contributions.shape[1]
    lower = jnp.concatenate(
        [contributions[i, width - w : width] for i, w in enumerate(widths)], 0
    )
    upper = jnp.concatenate(
        [contributions[i, size - width : size - width + w] for i, w in enumerate(widths)], 0
    )
    lower, upper = lax.optimization_barrier((lower, upper))
    from_above = from_behind(lower, "gz", -1)
    from_below = from_behind(upper, "gz", 1)
    cuts = [sum(widths[:i]) for i in range(len(widths) + 1)]
    below = jnp.stack(
        [
            jnp.pad(from_below[cuts[i] : cuts[i + 1]], ((0, width - w), (0, 0), (0, 0)))
            for i, w in enumerate(widths)
        ]
    )
    above = jnp.stack(
        [
            jnp.pad(from_above[cuts[i] : cuts[i + 1]], ((width - w, 0), (0, 0), (0, 0)))
            for i, w in enumerate(widths)
        ]
    )
    middle = contributions[:, width : size - width]
    inner = size - 2 * width
    return jnp.concatenate(
        (
            middle[:, :width] + below,
            middle[:, width : inner - width],
            middle[:, inner - width :] + above,
        ),
        axis=1,
    )


def packed_y_halo(cells):
    depth, rows = cells.shape[1], cells.shape[2]

    def rims(lo, hi, narrow):
        return jnp.concatenate(
            (
                cells[0, :, lo:hi],
                jnp.concatenate(
                    (cells[1, 2 : depth - 2, narrow], cells[2, 2 : depth - 2, narrow]), axis=1
                ),
            ),
            axis=0,
        )

    lower = rims(0, 4, slice(0, 2))
    upper = rims(rows - 4, rows, slice(rows - 2, rows))
    lower, upper = lax.optimization_barrier((lower, upper))
    from_above = from_behind(lower, "gy", -1)
    from_below = from_behind(upper, "gy", 1)

    def unpack(arrived, outer):
        narrow = arrived[depth:]
        spread = ((2, 2), outer, (0, 0))
        return jnp.stack(
            (
                arrived[:depth],
                jnp.pad(narrow[:, :2], spread),
                jnp.pad(narrow[:, 2:], spread),
            )
        )

    return jnp.concatenate(
        (unpack(from_below, (2, 0)), cells, unpack(from_above, (0, 2))), axis=2
    )


def packed_y_fold(contributions):
    depth, rows = contributions.shape[1], contributions.shape[2]

    half = (depth - 4) // 2

    def rims(lo, hi, narrow):
        third = contributions[2, 2 : depth - 2, narrow]
        return jnp.concatenate(
            (
                contributions[0, :, lo:hi],
                contributions[1, 1 : depth - 1, lo:hi],
                jnp.concatenate((third[:half], third[half:]), axis=1),
            ),
            axis=0,
        )

    lower = rims(0, 4, slice(2, 4))
    upper = rims(rows - 4, rows, slice(rows - 4, rows - 2))
    lower, upper = lax.optimization_barrier((lower, upper))
    from_above = from_behind(lower, "gy", -1)
    from_below = from_behind(upper, "gy", 1)

    def unpack(arrived, outer):
        third = arrived[2 * depth - 2 :]
        third = jnp.concatenate((third[:, :2], third[:, 2:]), axis=0)
        return jnp.stack(
            (
                arrived[:depth],
                jnp.pad(arrived[depth : 2 * depth - 2], ((1, 1), (0, 0), (0, 0))),
                jnp.pad(third, ((2, 2), outer, (0, 0))),
            )
        )

    middle = contributions[:, :, 4 : rows - 4]
    return jnp.concatenate(
        (
            middle[:, :, :4] + unpack(from_below, (0, 2)),
            middle[:, :, 4:-4],
            middle[:, :, -4:] + unpack(from_above, (2, 0)),
        ),
        axis=2,
    )


def advance_solver_step(phase_wide, temp_wide, kinetic_rate_field):
    padded = jnp.pad(phase_wide, ((0, 0), (0, 0), (2, 2)))
    grad_z = 0.5 * (padded[2:, 1:-1, 1:-1] - padded[:-2, 1:-1, 1:-1])
    grad_y = 0.5 * (padded[1:-1, 2:, 1:-1] - padded[1:-1, :-2, 1:-1])
    grad_x = 0.5 * (padded[1:-1, 1:-1, 2:] - padded[1:-1, 1:-1, :-2])
    sq_z = grad_z * grad_z
    sq_y = grad_y * grad_y
    sq_x = grad_x * grad_x
    squared = sq_z + sq_y + sq_x + GRAD_FLOOR
    quartic = (sq_z * sq_z + sq_y * sq_y + sq_x * sq_x) / (squared * squared)
    anisotropy = 1.0 + ANISOTROPY * (4.0 * quartic - 3.0)
    aniso_sq = anisotropy * anisotropy
    factor_a = 16.0 * ANISOTROPY * anisotropy / squared
    flux_z = ENERGY_SCALE * (aniso_sq * grad_z + factor_a * grad_z * (sq_z - quartic * squared))
    flux_y = ENERGY_SCALE * (aniso_sq * grad_y + factor_a * grad_y * (sq_y - quartic * squared))
    flux_x = ENERGY_SCALE * (aniso_sq * grad_x + factor_a * grad_x * (sq_x - quartic * squared))
    divergence = 0.5 * (flux_z[2:, 1:-1, 1:-1] - flux_z[:-2, 1:-1, 1:-1])
    divergence = divergence + 0.5 * (flux_y[1:-1, 2:, 1:-1] - flux_y[1:-1, :-2, 1:-1])
    divergence = divergence + 0.5 * (flux_x[1:-1, 1:-1, 2:] - flux_x[1:-1, 1:-1, :-2])
    phase_now = phase_wide[2:-2, 2:-2]
    temp_now = temp_wide[2:-2, 2:-2]
    driving = DRIVE_SCALE / jnp.pi * jnp.arctan(DRIVE_SHARP * (MELT_POINT - temp_now))
    growth = kinetic_rate_field * (
        divergence + phase_now * (1.0 - phase_now) * (phase_now - 0.5 + driving)
    )
    new_phase = phase_now + TIME_STEP * growth
    temp_x = jnp.pad(temp_now, ((0, 0), (0, 0), (1, 1)))
    laplacian = (
        temp_wide[3:-1, 2:-2]
        + temp_wide[1:-3, 2:-2]
        + temp_wide[2:-2, 3:-1]
        + temp_wide[2:-2, 1:-3]
    )
    laplacian = laplacian + temp_x[:, :, 2:] + temp_x[:, :, :-2] - 6.0 * temp_now
    new_temp = temp_now + TIME_STEP * laplacian + LATENT_HEAT * (new_phase - phase_now)
    return (new_phase, new_temp)


def fold_rims(contributions, width, sides):
    for axis, dim in sides:
        size = contributions.shape[dim]
        lower_rim = lax.slice_in_dim(contributions, 0, width, axis=dim)
        upper_rim = lax.slice_in_dim(contributions, size - width, size, axis=dim)
        middle = lax.slice_in_dim(contributions, width, size - width, axis=dim)
        inner = size - 2 * width
        lower_rim, upper_rim = lax.optimization_barrier((lower_rim, upper_rim))
        from_above = from_behind(lower_rim, axis, -1)
        from_below = from_behind(upper_rim, axis, 1)
        contributions = jnp.concatenate(
            (
                lax.slice_in_dim(middle, 0, width, axis=dim) + from_below,
                lax.slice_in_dim(middle, width, inner - width, axis=dim),
                lax.slice_in_dim(middle, inner - width, inner, axis=dim) + from_above,
            ),
            axis=dim,
        )
    return contributions


def inside_grid(cells, margin):
    nz, ny = cells.shape[0] - 2 * margin, cells.shape[1] - 2 * margin
    z = lax.axis_index("gz") * nz - margin + lax.broadcasted_iota(jnp.int32, cells.shape, 0)
    y = lax.axis_index("gy") * ny - margin + lax.broadcasted_iota(jnp.int32, cells.shape, 1)
    total_z = nz * lax.axis_size("gz")
    total_y = ny * lax.axis_size("gy")
    return (z >= 0) & (z < total_z) & (y >= 0) & (y < total_y)


def body(
    saved_order_parameter,
    saved_heat_level,
    kinetic_rate_field,
    order_parameter_adjoint_seed,
    heat_level_adjoint_seed,
):
    state = packed_z_halo(
        (saved_order_parameter, saved_heat_level, kinetic_rate_field), (4, 2, 2)
    )
    state = packed_y_halo(state)
    phase_wide, temp_wide, rate_wide = state[0], state[1], state[2]
    succeeding_order_parameter, succeeding_heat_level = advance_solver_step(
        phase_wide, temp_wide, rate_wide[2:-2, 2:-2]
    )
    valid = inside_grid(succeeding_order_parameter, 2)
    discarded_result, sensitivity_latest = jax.vjp(
        advance_solver_step,
        succeeding_order_parameter,
        succeeding_heat_level,
        rate_wide[4:-4, 4:-4],
    )
    halfway_order_parameter, halfway_heat_level, latest_kinetic_rate = sensitivity_latest(
        (order_parameter_adjoint_seed, heat_level_adjoint_seed)
    )
    halfway_order_parameter = jnp.where(valid, halfway_order_parameter, 0.0)
    halfway_heat_level = jnp.where(valid, halfway_heat_level, 0.0)
    discarded_result, prior_backward_sweep = jax.vjp(
        advance_solver_step, phase_wide, temp_wide, rate_wide[2:-2, 2:-2]
    )
    sensitivity_order_parameter, sensitivity_heat_level, early_mob = prior_backward_sweep(
        (halfway_order_parameter, halfway_heat_level)
    )
    early_mob = jnp.pad(early_mob, ((2, 2), (2, 2), (0, 0)))
    folded = packed_y_fold(
        jnp.stack((sensitivity_order_parameter, sensitivity_heat_level, early_mob))
    )
    folded = packed_z_fold(folded, (4, 3, 2))
    return (folded[0], folded[1], latest_kinetic_rate + folded[2])


def solution(mesh):
    return jax.shard_map(
        body,
        mesh=mesh,
        in_specs=(
            P("gz", "gy", None),
            P("gz", "gy", None),
            P("gz", "gy", None),
            P("gz", "gy", None),
            P("gz", "gy", None),
        ),
        out_specs=(P("gz", "gy", None), P("gz", "gy", None), P("gz", "gy", None)),
        check_vma=False,
    )
```

```python
import jax
import jax.numpy as jnp
from jax import lax
from jax.sharding import PartitionSpec as P

TIME_STEP = 0.15
ENERGY_SCALE = 0.5
ANISOTROPY = 0.05
GRAD_FLOOR = 0.01
LATENT_HEAT = 1.8
DRIVE_SCALE = 0.9
DRIVE_SHARP = 10.0
MELT_POINT = 1.0


def from_behind(block, axis, distance):
    devices = range(lax.axis_size(axis))
    route = [(i - distance, i) for i in devices if i - distance in devices]
    return lax.ppermute(block, axis, route)


def extended(cells, sides, width):
    for axis, dim in sides:
        count = lax.axis_size(axis)
        ends = count - 1
        head = lax.slice_in_dim(cells, 0, width, axis=dim)
        tail = lax.slice_in_dim(cells, cells.shape[dim] - width, cells.shape[dim], axis=dim)
        cells = jnp.concatenate(
            [
                lax.ppermute(tail, axis, [(i, (i + 1) % count) for i in range(ends)]),
                cells,
                lax.ppermute(head, axis, [((i + 1) % count, i) for i in range(ends)]),
            ],
            axis=dim,
        )
    return cells


def packed_z_halo(fields, widths):
    width, size = max(widths), fields[0].shape[0]
    tails = jnp.concatenate([f[size - w :] for f, w in zip(fields, widths)], 0)
    heads = jnp.concatenate([f[:w] for f, w in zip(fields, widths)], 0)
    cells = jnp.stack(fields)
    from_below = from_behind(tails, "gz", 1)
    from_above = from_behind(heads, "gz", -1)
    cuts = [sum(widths[:i]) for i in range(len(widths) + 1)]
    below = jnp.stack(
        [
            jnp.pad(from_below[cuts[i] : cuts[i + 1]], ((width - w, 0), (0, 0), (0, 0)))
            for i, w in enumerate(widths)
        ]
    )
    above = jnp.stack(
        [
            jnp.pad(from_above[cuts[i] : cuts[i + 1]], ((0, width - w), (0, 0), (0, 0)))
            for i, w in enumerate(widths)
        ]
    )
    return jnp.concatenate((below, cells, above), axis=1)


def packed_z_fold(contributions, widths):
    width, size = max(widths), contributions.shape[1]
    lower = jnp.concatenate(
        [contributions[i, width - w : width] for i, w in enumerate(widths)], 0
    )
    upper = jnp.concatenate(
        [contributions[i, size - width : size - width + w] for i, w in enumerate(widths)], 0
    )
    lower, upper = lax.optimization_barrier((lower, upper))
    from_above = from_behind(lower, "gz", -1)
    from_below = from_behind(upper, "gz", 1)
    cuts = [sum(widths[:i]) for i in range(len(widths) + 1)]
    below = jnp.stack(
        [
            jnp.pad(from_below[cuts[i] : cuts[i + 1]], ((0, width - w), (0, 0), (0, 0)))
            for i, w in enumerate(widths)
        ]
    )
    above = jnp.stack(
        [
            jnp.pad(from_above[cuts[i] : cuts[i + 1]], ((width - w, 0), (0, 0), (0, 0)))
            for i, w in enumerate(widths)
        ]
    )
    middle = contributions[:, width : size - width]
    inner = size - 2 * width
    return jnp.concatenate(
        (
            middle[:, :width] + below,
            middle[:, width : inner - width],
            middle[:, inner - width :] + above,
        ),
        axis=1,
    )


def packed_y_halo(cells):
    depth, rows = cells.shape[1], cells.shape[2]

    def rims(lo, hi, narrow):
        return jnp.concatenate(
            (
                cells[0, :, lo:hi],
                jnp.concatenate(
                    (cells[1, 2 : depth - 2, narrow], cells[2, 2 : depth - 2, narrow]), axis=1
                ),
            ),
            axis=0,
        )

    lower = rims(0, 4, slice(0, 2))
    upper = rims(rows - 4, rows, slice(rows - 2, rows))
    lower, upper = lax.optimization_barrier((lower, upper))
    from_above = from_behind(lower, "gy", -1)
    from_below = from_behind(upper, "gy", 1)

    def unpack(arrived, outer):
        narrow = arrived[depth:]
        spread = ((2, 2), outer, (0, 0))
        return jnp.stack(
            (
                arrived[:depth],
                jnp.pad(narrow[:, :2], spread),
                jnp.pad(narrow[:, 2:], spread),
            )
        )

    return jnp.concatenate(
        (unpack(from_below, (2, 0)), cells, unpack(from_above, (0, 2))), axis=2
    )


def packed_y_fold(contributions):
    depth, rows = contributions.shape[1], contributions.shape[2]

    half = (depth - 4) // 2

    def rims(lo, hi, narrow):
        third = contributions[2, 2 : depth - 2, narrow]
        return jnp.concatenate(
            (
                contributions[0, :, lo:hi],
                contributions[1, 1 : depth - 1, lo:hi],
                jnp.concatenate((third[:half], third[half:]), axis=1),
            ),
            axis=0,
        )

    lower = rims(0, 4, slice(2, 4))
    upper = rims(rows - 4, rows, slice(rows - 4, rows - 2))
    lower, upper = lax.optimization_barrier((lower, upper))
    from_above = from_behind(lower, "gy", -1)
    from_below = from_behind(upper, "gy", 1)

    def unpack(arrived, outer):
        third = arrived[2 * depth - 2 :]
        third = jnp.concatenate((third[:, :2], third[:, 2:]), axis=0)
        return jnp.stack(
            (
                arrived[:depth],
                jnp.pad(arrived[depth : 2 * depth - 2], ((1, 1), (0, 0), (0, 0))),
                jnp.pad(third, ((2, 2), outer, (0, 0))),
            )
        )

    middle = contributions[:, :, 4 : rows - 4]
    return jnp.concatenate(
        (
            middle[:, :, :4] + unpack(from_below, (0, 2)),
            middle[:, :, 4:-4],
            middle[:, :, -4:] + unpack(from_above, (2, 0)),
        ),
        axis=2,
    )


def fluxes(grad_z, grad_y, grad_x):
    sq_z = grad_z * grad_z
    sq_y = grad_y * grad_y
    sq_x = grad_x * grad_x
    squared = sq_z + sq_y + sq_x + GRAD_FLOOR
    quartic = (sq_z * sq_z + sq_y * sq_y + sq_x * sq_x) / (squared * squared)
    anisotropy = 1.0 + ANISOTROPY * (4.0 * quartic - 3.0)
    aniso_sq = anisotropy * anisotropy
    factor_a = 16.0 * ANISOTROPY * anisotropy / squared
    flux_z = ENERGY_SCALE * (aniso_sq * grad_z + factor_a * grad_z * (sq_z - quartic * squared))
    flux_y = ENERGY_SCALE * (aniso_sq * grad_y + factor_a * grad_y * (sq_y - quartic * squared))
    flux_x = ENERGY_SCALE * (aniso_sq * grad_x + factor_a * grad_x * (sq_x - quartic * squared))
    return flux_z, flux_y, flux_x


def advance_solver_step(phase_wide, temp_wide, kinetic_rate_field):
    cells = phase_wide[1:-1, 1:-1]
    none = jnp.zeros_like(cells[:, :, :1])
    grad_z = 0.5 * (phase_wide[2:, 1:-1] - phase_wide[:-2, 1:-1])
    grad_y = 0.5 * (phase_wide[1:-1, 2:] - phase_wide[1:-1, :-2])
    grad_x = 0.5 * (
        jnp.concatenate((cells[:, :, 1:], none), axis=2)
        - jnp.concatenate((none, cells[:, :, :-1]), axis=2)
    )
    flux_z, flux_y, flux_x = fluxes(grad_z, grad_y, grad_x)
    phase_now = phase_wide[2:-2, 2:-2]
    edge_x = jnp.stack((0.5 * (phase_now[:, :, 0] - 0.0), 0.5 * (0.0 - phase_now[:, :, -1])))
    edge_zero = jnp.zeros_like(edge_x)
    edge_flux = fluxes(edge_zero, edge_zero, edge_x)[2]
    inner_x = flux_x[1:-1, 1:-1]
    ahead = jnp.concatenate((inner_x[:, :, 1:], edge_flux[1][:, :, None]), axis=2)
    behind = jnp.concatenate((edge_flux[0][:, :, None], inner_x[:, :, :-1]), axis=2)
    divergence = 0.5 * (flux_z[2:, 1:-1] - flux_z[:-2, 1:-1])
    divergence = divergence + 0.5 * (flux_y[1:-1, 2:] - flux_y[1:-1, :-2])
    divergence = divergence + 0.5 * (ahead - behind)
    temp_now = temp_wide[2:-2, 2:-2]
    driving = DRIVE_SCALE / jnp.pi * jnp.arctan(DRIVE_SHARP * (MELT_POINT - temp_now))
    growth = kinetic_rate_field * (
        divergence + phase_now * (1.0 - phase_now) * (phase_now - 0.5 + driving)
    )
    new_phase = phase_now + TIME_STEP * growth
    temp_x = jnp.pad(temp_now, ((0, 0), (0, 0), (1, 1)))
    laplacian = (
        temp_wide[3:-1, 2:-2]
        + temp_wide[1:-3, 2:-2]
        + temp_wide[2:-2, 3:-1]
        + temp_wide[2:-2, 1:-3]
    )
    laplacian = laplacian + temp_x[:, :, 2:] + temp_x[:, :, :-2] - 6.0 * temp_now
    new_temp = temp_now + TIME_STEP * laplacian + LATENT_HEAT * (new_phase - phase_now)
    return (new_phase, new_temp)


def fold_rims(contributions, width, sides):
    for axis, dim in sides:
        size = contributions.shape[dim]
        lower_rim = lax.slice_in_dim(contributions, 0, width, axis=dim)
        upper_rim = lax.slice_in_dim(contributions, size - width, size, axis=dim)
        middle = lax.slice_in_dim(contributions, width, size - width, axis=dim)
        inner = size - 2 * width
        lower_rim, upper_rim = lax.optimization_barrier((lower_rim, upper_rim))
        from_above = from_behind(lower_rim, axis, -1)
        from_below = from_behind(upper_rim, axis, 1)
        contributions = jnp.concatenate(
            (
                lax.slice_in_dim(middle, 0, width, axis=dim) + from_below,
                lax.slice_in_dim(middle, width, inner - width, axis=dim),
                lax.slice_in_dim(middle, inner - width, inner, axis=dim) + from_above,
            ),
            axis=dim,
        )
    return contributions


def inside_grid(cells, margin):
    nz, ny = cells.shape[0] - 2 * margin, cells.shape[1] - 2 * margin
    z = lax.axis_index("gz") * nz - margin + lax.broadcasted_iota(jnp.int32, cells.shape, 0)
    y = lax.axis_index("gy") * ny - margin + lax.broadcasted_iota(jnp.int32, cells.shape, 1)
    total_z = nz * lax.axis_size("gz")
    total_y = ny * lax.axis_size("gy")
    return (z >= 0) & (z < total_z) & (y >= 0) & (y < total_y)


def body(
    saved_order_parameter,
    saved_heat_level,
    kinetic_rate_field,
    order_parameter_adjoint_seed,
    heat_level_adjoint_seed,
):
    state = packed_z_halo(
        (saved_order_parameter, saved_heat_level, kinetic_rate_field), (4, 2, 2)
    )
    state = packed_y_halo(state)
    phase_wide, temp_wide, rate_wide = state[0], state[1], state[2]
    succeeding_order_parameter, succeeding_heat_level = advance_solver_step(
        phase_wide, temp_wide, rate_wide[2:-2, 2:-2]
    )
    valid = inside_grid(succeeding_order_parameter, 2)
    discarded_result, sensitivity_latest = jax.vjp(
        advance_solver_step,
        succeeding_order_parameter,
        succeeding_heat_level,
        rate_wide[4:-4, 4:-4],
    )
    halfway_order_parameter, halfway_heat_level, latest_kinetic_rate = sensitivity_latest(
        (order_parameter_adjoint_seed, heat_level_adjoint_seed)
    )
    halfway_order_parameter = jnp.where(valid, halfway_order_parameter, 0.0)
    halfway_heat_level = jnp.where(valid, halfway_heat_level, 0.0)
    discarded_result, prior_backward_sweep = jax.vjp(
        advance_solver_step, phase_wide, temp_wide, rate_wide[2:-2, 2:-2]
    )
    sensitivity_order_parameter, sensitivity_heat_level, early_mob = prior_backward_sweep(
        (halfway_order_parameter, halfway_heat_level)
    )
    early_mob = jnp.pad(early_mob, ((2, 2), (2, 2), (0, 0)))
    folded = packed_y_fold(
        jnp.stack((sensitivity_order_parameter, sensitivity_heat_level, early_mob))
    )
    folded = packed_z_fold(folded, (4, 3, 2))
    return (folded[0], folded[1], latest_kinetic_rate + folded[2])


def solution(mesh):
    return jax.shard_map(
        body,
        mesh=mesh,
        in_specs=(
            P("gz", "gy", None),
            P("gz", "gy", None),
            P("gz", "gy", None),
            P("gz", "gy", None),
            P("gz", "gy", None),
        ),
        out_specs=(P("gz", "gy", None), P("gz", "gy", None), P("gz", "gy", None)),
        check_vma=False,
    )
```

```python
import jax
import jax.numpy as jnp
from jax import lax
from jax.sharding import PartitionSpec as P

TIME_STEP = 0.15
ENERGY_SCALE = 0.5
ANISOTROPY = 0.05
GRAD_FLOOR = 0.01
LATENT_HEAT = 1.8
DRIVE_SCALE = 0.9
DRIVE_SHARP = 10.0
MELT_POINT = 1.0


def from_behind(block, axis, distance):
    devices = range(lax.axis_size(axis))
    route = [(i - distance, i) for i in devices if i - distance in devices]
    return lax.ppermute(block, axis, route)


def extended(cells, sides, width):
    for axis, dim in sides:
        count = lax.axis_size(axis)
        ends = count - 1
        head = lax.slice_in_dim(cells, 0, width, axis=dim)
        tail = lax.slice_in_dim(cells, cells.shape[dim] - width, cells.shape[dim], axis=dim)
        cells = jnp.concatenate(
            [
                lax.ppermute(tail, axis, [(i, (i + 1) % count) for i in range(ends)]),
                cells,
                lax.ppermute(head, axis, [((i + 1) % count, i) for i in range(ends)]),
            ],
            axis=dim,
        )
    return cells


def packed_z_halo(fields, widths):
    width, size = max(widths), fields[0].shape[0]
    tails = jnp.concatenate([f[size - w :] for f, w in zip(fields, widths)], 0)
    heads = jnp.concatenate([f[:w] for f, w in zip(fields, widths)], 0)
    cells = jnp.stack(fields)
    from_below = from_behind(tails, "gz", 1)
    from_above = from_behind(heads, "gz", -1)
    cuts = [sum(widths[:i]) for i in range(len(widths) + 1)]
    below = jnp.stack(
        [
            jnp.pad(from_below[cuts[i] : cuts[i + 1]], ((width - w, 0), (0, 0), (0, 0)))
            for i, w in enumerate(widths)
        ]
    )
    above = jnp.stack(
        [
            jnp.pad(from_above[cuts[i] : cuts[i + 1]], ((0, width - w), (0, 0), (0, 0)))
            for i, w in enumerate(widths)
        ]
    )
    return jnp.concatenate((below, cells, above), axis=1)


def packed_z_fold(contributions, widths):
    width, size = max(widths), contributions.shape[1]
    lower = jnp.concatenate(
        [contributions[i, width - w : width] for i, w in enumerate(widths)], 0
    )
    upper = jnp.concatenate(
        [contributions[i, size - width : size - width + w] for i, w in enumerate(widths)], 0
    )
    lower, upper = lax.optimization_barrier((lower, upper))
    from_above = from_behind(lower, "gz", -1)
    from_below = from_behind(upper, "gz", 1)
    cuts = [sum(widths[:i]) for i in range(len(widths) + 1)]
    below = jnp.stack(
        [
            jnp.pad(from_below[cuts[i] : cuts[i + 1]], ((0, width - w), (0, 0), (0, 0)))
            for i, w in enumerate(widths)
        ]
    )
    above = jnp.stack(
        [
            jnp.pad(from_above[cuts[i] : cuts[i + 1]], ((width - w, 0), (0, 0), (0, 0)))
            for i, w in enumerate(widths)
        ]
    )
    middle = contributions[:, width : size - width]
    inner = size - 2 * width
    return jnp.concatenate(
        (
            middle[:, :width] + below,
            middle[:, width : inner - width],
            middle[:, inner - width :] + above,
        ),
        axis=1,
    )


def packed_y_halo(cells):
    depth, rows = cells.shape[1], cells.shape[2]

    def rims(lo, hi, narrow):
        return jnp.concatenate(
            (
                cells[0, :, lo:hi],
                jnp.concatenate(
                    (cells[1, 2 : depth - 2, narrow], cells[2, 2 : depth - 2, narrow]), axis=1
                ),
            ),
            axis=0,
        )

    lower = rims(0, 4, slice(0, 2))
    upper = rims(rows - 4, rows, slice(rows - 2, rows))
    lower, upper = lax.optimization_barrier((lower, upper))
    from_above = from_behind(lower, "gy", -1)
    from_below = from_behind(upper, "gy", 1)

    def unpack(arrived, outer):
        narrow = arrived[depth:]
        spread = ((2, 2), outer, (0, 0))
        return jnp.stack(
            (
                arrived[:depth],
                jnp.pad(narrow[:, :2], spread),
                jnp.pad(narrow[:, 2:], spread),
            )
        )

    return jnp.concatenate(
        (unpack(from_below, (2, 0)), cells, unpack(from_above, (0, 2))), axis=2
    )


def packed_y_fold(contributions):
    depth, rows = contributions.shape[1], contributions.shape[2]
    quarter = (depth - 4) // 4

    def rims(second_rows, third_first, third_second):
        second = contributions[1, 1 : depth - 1, second_rows]
        third = contributions[2, 2 : depth - 2]
        first_row = third[:, third_first : third_first + 1]
        second_row = jnp.pad(third[:, third_second : third_second + 1], ((1, 1), (0, 0), (0, 0)))
        return jnp.concatenate(
            (
                jnp.concatenate((second, second_row), axis=1),
                jnp.concatenate(
                    [first_row[k * quarter : (k + 1) * quarter] for k in range(4)], axis=1
                ),
            ),
            axis=0,
        )

    lower = jnp.concatenate(
        (contributions[0, :, 0:4], rims(slice(1, 4), 2, 3)), axis=0
    )
    upper = jnp.concatenate(
        (contributions[0, :, rows - 4 :], rims(slice(rows - 4, rows - 1), rows - 4, rows - 3)),
        axis=0,
    )
    lower, upper = lax.optimization_barrier((lower, upper))
    from_above = from_behind(lower, "gy", -1)
    from_below = from_behind(upper, "gy", 1)

    def unpack(arrived, second_side, third_side):
        block = arrived[depth : 2 * depth - 2]
        spread = arrived[2 * depth - 2 :]
        second = jnp.pad(block[:, 0:3], ((1, 1), second_side, (0, 0)))
        first_row = jnp.concatenate([spread[:, k : k + 1] for k in range(4)], axis=0)
        third = jnp.concatenate((first_row, block[1 : depth - 3, 3:4]), axis=1)
        third = jnp.pad(third, ((2, 2), third_side, (0, 0)))
        return jnp.stack((arrived[:depth], second, third))

    middle = contributions[:, :, 4 : rows - 4]
    return jnp.concatenate(
        (
            middle[:, :, :4] + unpack(from_below, (0, 1), (0, 2)),
            middle[:, :, 4:-4],
            middle[:, :, -4:] + unpack(from_above, (1, 0), (2, 0)),
        ),
        axis=2,
    )


def advance_solver_step(phase_wide, temp_wide, kinetic_rate_field):
    padded = jnp.pad(phase_wide, ((0, 0), (0, 0), (2, 2)))
    grad_z = 0.5 * (padded[2:, 1:-1, 1:-1] - padded[:-2, 1:-1, 1:-1])
    grad_y = 0.5 * (padded[1:-1, 2:, 1:-1] - padded[1:-1, :-2, 1:-1])
    grad_x = 0.5 * (padded[1:-1, 1:-1, 2:] - padded[1:-1, 1:-1, :-2])
    sq_z = grad_z * grad_z
    sq_y = grad_y * grad_y
    sq_x = grad_x * grad_x
    squared = sq_z + sq_y + sq_x + GRAD_FLOOR
    quartic = (sq_z * sq_z + sq_y * sq_y + sq_x * sq_x) / (squared * squared)
    anisotropy = 1.0 + ANISOTROPY * (4.0 * quartic - 3.0)
    aniso_sq = anisotropy * anisotropy
    factor_a = 16.0 * ANISOTROPY * anisotropy / squared
    flux_z = ENERGY_SCALE * (aniso_sq * grad_z + factor_a * grad_z * (sq_z - quartic * squared))
    flux_y = ENERGY_SCALE * (aniso_sq * grad_y + factor_a * grad_y * (sq_y - quartic * squared))
    flux_x = ENERGY_SCALE * (aniso_sq * grad_x + factor_a * grad_x * (sq_x - quartic * squared))
    divergence = 0.5 * (flux_z[2:, 1:-1, 1:-1] - flux_z[:-2, 1:-1, 1:-1])
    divergence = divergence + 0.5 * (flux_y[1:-1, 2:, 1:-1] - flux_y[1:-1, :-2, 1:-1])
    divergence = divergence + 0.5 * (flux_x[1:-1, 1:-1, 2:] - flux_x[1:-1, 1:-1, :-2])
    phase_now = phase_wide[2:-2, 2:-2]
    temp_now = temp_wide[2:-2, 2:-2]
    driving = DRIVE_SCALE / jnp.pi * jnp.arctan(DRIVE_SHARP * (MELT_POINT - temp_now))
    growth = kinetic_rate_field * (
        divergence + phase_now * (1.0 - phase_now) * (phase_now - 0.5 + driving)
    )
    new_phase = phase_now + TIME_STEP * growth
    temp_x = jnp.pad(temp_now, ((0, 0), (0, 0), (1, 1)))
    laplacian = (
        temp_wide[3:-1, 2:-2]
        + temp_wide[1:-3, 2:-2]
        + temp_wide[2:-2, 3:-1]
        + temp_wide[2:-2, 1:-3]
    )
    laplacian = laplacian + temp_x[:, :, 2:] + temp_x[:, :, :-2] - 6.0 * temp_now
    new_temp = temp_now + TIME_STEP * laplacian + LATENT_HEAT * (new_phase - phase_now)
    return (new_phase, new_temp)


def fold_rims(contributions, width, sides):
    for axis, dim in sides:
        size = contributions.shape[dim]
        lower_rim = lax.slice_in_dim(contributions, 0, width, axis=dim)
        upper_rim = lax.slice_in_dim(contributions, size - width, size, axis=dim)
        middle = lax.slice_in_dim(contributions, width, size - width, axis=dim)
        inner = size - 2 * width
        lower_rim, upper_rim = lax.optimization_barrier((lower_rim, upper_rim))
        from_above = from_behind(lower_rim, axis, -1)
        from_below = from_behind(upper_rim, axis, 1)
        contributions = jnp.concatenate(
            (
                lax.slice_in_dim(middle, 0, width, axis=dim) + from_below,
                lax.slice_in_dim(middle, width, inner - width, axis=dim),
                lax.slice_in_dim(middle, inner - width, inner, axis=dim) + from_above,
            ),
            axis=dim,
        )
    return contributions


def inside_grid(cells, margin):
    nz, ny = cells.shape[0] - 2 * margin, cells.shape[1] - 2 * margin
    z = lax.axis_index("gz") * nz - margin + lax.broadcasted_iota(jnp.int32, cells.shape, 0)
    y = lax.axis_index("gy") * ny - margin + lax.broadcasted_iota(jnp.int32, cells.shape, 1)
    total_z = nz * lax.axis_size("gz")
    total_y = ny * lax.axis_size("gy")
    return (z >= 0) & (z < total_z) & (y >= 0) & (y < total_y)


def body(
    saved_order_parameter,
    saved_heat_level,
    kinetic_rate_field,
    order_parameter_adjoint_seed,
    heat_level_adjoint_seed,
):
    state = packed_z_halo(
        (saved_order_parameter, saved_heat_level, kinetic_rate_field), (4, 2, 2)
    )
    state = packed_y_halo(state)
    phase_wide, temp_wide, rate_wide = state[0], state[1], state[2]
    succeeding_order_parameter, succeeding_heat_level = advance_solver_step(
        phase_wide, temp_wide, rate_wide[2:-2, 2:-2]
    )
    valid = inside_grid(succeeding_order_parameter, 2)
    discarded_result, sensitivity_latest = jax.vjp(
        advance_solver_step,
        succeeding_order_parameter,
        succeeding_heat_level,
        rate_wide[4:-4, 4:-4],
    )
    halfway_order_parameter, halfway_heat_level, latest_kinetic_rate = sensitivity_latest(
        (order_parameter_adjoint_seed, heat_level_adjoint_seed)
    )
    halfway_order_parameter = jnp.where(valid, halfway_order_parameter, 0.0)
    halfway_heat_level = jnp.where(valid, halfway_heat_level, 0.0)
    discarded_result, prior_backward_sweep = jax.vjp(
        advance_solver_step, phase_wide, temp_wide, rate_wide[2:-2, 2:-2]
    )
    sensitivity_order_parameter, sensitivity_heat_level, early_mob = prior_backward_sweep(
        (halfway_order_parameter, halfway_heat_level)
    )
    early_mob = jnp.pad(early_mob, ((2, 2), (2, 2), (0, 0)))
    folded = packed_y_fold(
        jnp.stack((sensitivity_order_parameter, sensitivity_heat_level, early_mob))
    )
    folded = packed_z_fold(folded, (4, 3, 2))
    return (folded[0], folded[1], latest_kinetic_rate + folded[2])


def solution(mesh):
    return jax.shard_map(
        body,
        mesh=mesh,
        in_specs=(
            P("gz", "gy", None),
            P("gz", "gy", None),
            P("gz", "gy", None),
            P("gz", "gy", None),
            P("gz", "gy", None),
        ),
        out_specs=(P("gz", "gy", None), P("gz", "gy", None), P("gz", "gy", None)),
        check_vma=False,
    )
```

```python
import jax
import jax.numpy as jnp
from jax import lax
from jax.sharding import PartitionSpec as P

TIME_STEP = 0.15
ENERGY_SCALE = 0.5
ANISOTROPY = 0.05
GRAD_FLOOR = 0.01
LATENT_HEAT = 1.8
DRIVE_SCALE = 0.9
DRIVE_SHARP = 10.0
MELT_POINT = 1.0


def from_behind(block, axis, distance):
    devices = range(lax.axis_size(axis))
    route = [(i - distance, i) for i in devices if i - distance in devices]
    return lax.ppermute(block, axis, route)


def extended(cells, sides, width):
    for axis, dim in sides:
        count = lax.axis_size(axis)
        ends = count - 1
        head = lax.slice_in_dim(cells, 0, width, axis=dim)
        tail = lax.slice_in_dim(cells, cells.shape[dim] - width, cells.shape[dim], axis=dim)
        cells = jnp.concatenate(
            [
                lax.ppermute(tail, axis, [(i, (i + 1) % count) for i in range(ends)]),
                cells,
                lax.ppermute(head, axis, [((i + 1) % count, i) for i in range(ends)]),
            ],
            axis=dim,
        )
    return cells


def packed_z_halo(fields, widths):
    width, size = max(widths), fields[0].shape[0]
    tails = jnp.concatenate([f[size - w :] for f, w in zip(fields, widths)], 0)
    heads = jnp.concatenate([f[:w] for f, w in zip(fields, widths)], 0)
    cells = jnp.stack(fields)
    from_below = from_behind(tails, "gz", 1)
    from_above = from_behind(heads, "gz", -1)
    cuts = [sum(widths[:i]) for i in range(len(widths) + 1)]
    below = jnp.stack(
        [
            jnp.pad(from_below[cuts[i] : cuts[i + 1]], ((width - w, 0), (0, 0), (0, 0)))
            for i, w in enumerate(widths)
        ]
    )
    above = jnp.stack(
        [
            jnp.pad(from_above[cuts[i] : cuts[i + 1]], ((0, width - w), (0, 0), (0, 0)))
            for i, w in enumerate(widths)
        ]
    )
    return jnp.concatenate((below, cells, above), axis=1)


def packed_z_fold(contributions, widths):
    width, size = max(widths), contributions.shape[1]
    lower = jnp.concatenate(
        [contributions[i, width - w : width] for i, w in enumerate(widths)], 0
    )
    upper = jnp.concatenate(
        [contributions[i, size - width : size - width + w] for i, w in enumerate(widths)], 0
    )
    lower, upper = lax.optimization_barrier((lower, upper))
    from_above = from_behind(lower, "gz", -1)
    from_below = from_behind(upper, "gz", 1)
    cuts = [sum(widths[:i]) for i in range(len(widths) + 1)]
    below = jnp.stack(
        [
            jnp.pad(from_below[cuts[i] : cuts[i + 1]], ((0, width - w), (0, 0), (0, 0)))
            for i, w in enumerate(widths)
        ]
    )
    above = jnp.stack(
        [
            jnp.pad(from_above[cuts[i] : cuts[i + 1]], ((width - w, 0), (0, 0), (0, 0)))
            for i, w in enumerate(widths)
        ]
    )
    middle = contributions[:, width : size - width]
    inner = size - 2 * width
    return jnp.concatenate(
        (
            middle[:, :width] + below,
            middle[:, width : inner - width],
            middle[:, inner - width :] + above,
        ),
        axis=1,
    )


def packed_y_halo(cells):
    depth, rows = cells.shape[1], cells.shape[2]

    def rims(lo, hi, narrow):
        return jnp.concatenate(
            (
                cells[0, :, lo:hi],
                jnp.concatenate(
                    (cells[1, 2 : depth - 2, narrow], cells[2, 2 : depth - 2, narrow]), axis=1
                ),
            ),
            axis=0,
        )

    lower = rims(0, 4, slice(0, 2))
    upper = rims(rows - 4, rows, slice(rows - 2, rows))
    lower, upper = lax.optimization_barrier((lower, upper))
    from_above = from_behind(lower, "gy", -1)
    from_below = from_behind(upper, "gy", 1)

    def unpack(arrived, outer):
        narrow = arrived[depth:]
        spread = ((2, 2), outer, (0, 0))
        return jnp.stack(
            (
                arrived[:depth],
                jnp.pad(narrow[:, :2], spread),
                jnp.pad(narrow[:, 2:], spread),
            )
        )

    return jnp.concatenate(
        (unpack(from_below, (2, 0)), cells, unpack(from_above, (0, 2))), axis=2
    )


def packed_y_fold(contributions):
    depth, rows = contributions.shape[1], contributions.shape[2]
    quarter = (depth - 4) // 4

    def rims(second_rows, third_first, third_second):
        second = contributions[1, 1 : depth - 1, second_rows]
        third = contributions[2, 2 : depth - 2]
        first_row = third[:, third_first : third_first + 1]
        second_row = jnp.pad(third[:, third_second : third_second + 1], ((1, 1), (0, 0), (0, 0)))
        return jnp.concatenate(
            (
                jnp.concatenate((second, second_row), axis=1),
                jnp.concatenate(
                    [first_row[k * quarter : (k + 1) * quarter] for k in range(4)], axis=1
                ),
            ),
            axis=0,
        )

    lower = jnp.concatenate(
        (contributions[0, :, 0:4], rims(slice(1, 4), 2, 3)), axis=0
    )
    upper = jnp.concatenate(
        (contributions[0, :, rows - 4 :], rims(slice(rows - 4, rows - 1), rows - 4, rows - 3)),
        axis=0,
    )
    lower, upper = lax.optimization_barrier((lower, upper))
    from_above = from_behind(lower, "gy", -1)
    from_below = from_behind(upper, "gy", 1)

    def unpack(arrived, second_side, third_side):
        block = arrived[depth : 2 * depth - 2]
        spread = arrived[2 * depth - 2 :]
        second = jnp.pad(block[:, 0:3], ((1, 1), second_side, (0, 0)))
        first_row = jnp.concatenate([spread[:, k : k + 1] for k in range(4)], axis=0)
        third = jnp.concatenate((first_row, block[1 : depth - 3, 3:4]), axis=1)
        third = jnp.pad(third, ((2, 2), third_side, (0, 0)))
        return jnp.stack((arrived[:depth], second, third))

    middle = contributions[:, :, 4 : rows - 4]
    return jnp.concatenate(
        (
            middle[:, :, :4] + unpack(from_below, (0, 1), (0, 2)),
            middle[:, :, 4:-4],
            middle[:, :, -4:] + unpack(from_above, (1, 0), (2, 0)),
        ),
        axis=2,
    )


def advance_solver_step(phase_wide, temp_wide, kinetic_rate_field):
    padded = jnp.pad(phase_wide, ((0, 0), (0, 0), (2, 2)))
    grad_z = 0.5 * (padded[2:, 1:-1, 1:-1] - padded[:-2, 1:-1, 1:-1])
    grad_y = 0.5 * (padded[1:-1, 2:, 1:-1] - padded[1:-1, :-2, 1:-1])
    grad_x = 0.5 * (padded[1:-1, 1:-1, 2:] - padded[1:-1, 1:-1, :-2])
    sq_z = grad_z * grad_z
    sq_y = grad_y * grad_y
    sq_x = grad_x * grad_x
    squared = sq_z + sq_y + sq_x + GRAD_FLOOR
    quartic = (sq_z * sq_z + sq_y * sq_y + sq_x * sq_x) / (squared * squared)
    anisotropy = 1.0 + ANISOTROPY * (4.0 * quartic - 3.0)
    aniso_sq = anisotropy * anisotropy
    factor_a = 16.0 * ANISOTROPY * anisotropy / squared
    flux_z = ENERGY_SCALE * (aniso_sq * grad_z + factor_a * grad_z * (sq_z - quartic * squared))
    flux_y = ENERGY_SCALE * (aniso_sq * grad_y + factor_a * grad_y * (sq_y - quartic * squared))
    flux_x = ENERGY_SCALE * (aniso_sq * grad_x + factor_a * grad_x * (sq_x - quartic * squared))
    divergence = 0.5 * (flux_z[2:, 1:-1, 1:-1] - flux_z[:-2, 1:-1, 1:-1])
    divergence = divergence + 0.5 * (flux_y[1:-1, 2:, 1:-1] - flux_y[1:-1, :-2, 1:-1])
    divergence = divergence + 0.5 * (flux_x[1:-1, 1:-1, 2:] - flux_x[1:-1, 1:-1, :-2])
    phase_now = phase_wide[2:-2, 2:-2]
    temp_now = temp_wide[2:-2, 2:-2]
    driving = DRIVE_SCALE / jnp.pi * jnp.arctan(DRIVE_SHARP * (MELT_POINT - temp_now))
    growth = kinetic_rate_field * (
        divergence + phase_now * (1.0 - phase_now) * (phase_now - 0.5 + driving)
    )
    new_phase = phase_now + TIME_STEP * growth
    temp_x = jnp.pad(temp_now, ((0, 0), (0, 0), (1, 1)))
    laplacian = (
        temp_wide[3:-1, 2:-2]
        + temp_wide[1:-3, 2:-2]
        + temp_wide[2:-2, 3:-1]
        + temp_wide[2:-2, 1:-3]
    )
    laplacian = laplacian + temp_x[:, :, 2:] + temp_x[:, :, :-2] - 6.0 * temp_now
    new_temp = temp_now + TIME_STEP * laplacian + LATENT_HEAT * (new_phase - phase_now)
    return (new_phase, new_temp)


def fold_rims(contributions, width, sides):
    for axis, dim in sides:
        size = contributions.shape[dim]
        lower_rim = lax.slice_in_dim(contributions, 0, width, axis=dim)
        upper_rim = lax.slice_in_dim(contributions, size - width, size, axis=dim)
        middle = lax.slice_in_dim(contributions, width, size - width, axis=dim)
        inner = size - 2 * width
        lower_rim, upper_rim = lax.optimization_barrier((lower_rim, upper_rim))
        from_above = from_behind(lower_rim, axis, -1)
        from_below = from_behind(upper_rim, axis, 1)
        contributions = jnp.concatenate(
            (
                lax.slice_in_dim(middle, 0, width, axis=dim) + from_below,
                lax.slice_in_dim(middle, width, inner - width, axis=dim),
                lax.slice_in_dim(middle, inner - width, inner, axis=dim) + from_above,
            ),
            axis=dim,
        )
    return contributions


def inside_grid(cells, margin):
    nz, ny = cells.shape[0] - 2 * margin, cells.shape[1] - 2 * margin
    z = lax.axis_index("gz") * nz - margin + lax.broadcasted_iota(jnp.int32, cells.shape, 0)
    y = lax.axis_index("gy") * ny - margin + lax.broadcasted_iota(jnp.int32, cells.shape, 1)
    total_z = nz * lax.axis_size("gz")
    total_y = ny * lax.axis_size("gy")
    return (z >= 0) & (z < total_z) & (y >= 0) & (y < total_y)


def body(
    saved_order_parameter,
    saved_heat_level,
    kinetic_rate_field,
    order_parameter_adjoint_seed,
    heat_level_adjoint_seed,
):
    state = packed_z_halo(
        (saved_order_parameter, saved_heat_level, kinetic_rate_field), (4, 2, 2)
    )
    state = packed_y_halo(state)
    phase_wide, temp_wide, rate_wide = state[0], state[1], state[2]
    succeeding_order_parameter, succeeding_heat_level = advance_solver_step(
        phase_wide, temp_wide, rate_wide[2:-2, 2:-2]
    )
    valid = inside_grid(succeeding_order_parameter, 2)
    discarded_result, sensitivity_latest = jax.vjp(
        advance_solver_step,
        succeeding_order_parameter,
        succeeding_heat_level,
        rate_wide[4:-4, 4:-4],
    )
    halfway_order_parameter, halfway_heat_level, latest_kinetic_rate = sensitivity_latest(
        (order_parameter_adjoint_seed, heat_level_adjoint_seed)
    )
    halfway_heat_level = jnp.where(valid, halfway_heat_level, 0.0)
    discarded_result, prior_backward_sweep = jax.vjp(
        advance_solver_step, phase_wide, temp_wide, rate_wide[2:-2, 2:-2]
    )
    sensitivity_order_parameter, sensitivity_heat_level, early_mob = prior_backward_sweep(
        (halfway_order_parameter, halfway_heat_level)
    )
    early_mob = jnp.pad(early_mob, ((2, 2), (2, 2), (0, 0)))
    folded = packed_y_fold(
        jnp.stack((sensitivity_order_parameter, sensitivity_heat_level, early_mob))
    )
    folded = packed_z_fold(folded, (4, 3, 2))
    return (folded[0], folded[1], latest_kinetic_rate + folded[2])


def solution(mesh):
    return jax.shard_map(
        body,
        mesh=mesh,
        in_specs=(
            P("gz", "gy", None),
            P("gz", "gy", None),
            P("gz", "gy", None),
            P("gz", "gy", None),
            P("gz", "gy", None),
        ),
        out_specs=(P("gz", "gy", None), P("gz", "gy", None), P("gz", "gy", None)),
        check_vma=False,
    )
```

```python
import jax
import jax.numpy as jnp
from jax import lax
from jax.sharding import PartitionSpec as P

TIME_STEP = 0.15
ENERGY_SCALE = 0.5
ANISOTROPY = 0.05
GRAD_FLOOR = 0.01
LATENT_HEAT = 1.8
DRIVE_SCALE = 0.9
DRIVE_SHARP = 10.0
MELT_POINT = 1.0


def from_behind(block, axis, distance):
    devices = range(lax.axis_size(axis))
    route = [(i - distance, i) for i in devices if i - distance in devices]
    return lax.ppermute(block, axis, route)


def extended(cells, sides, width):
    for axis, dim in sides:
        count = lax.axis_size(axis)
        ends = count - 1
        head = lax.slice_in_dim(cells, 0, width, axis=dim)
        tail = lax.slice_in_dim(cells, cells.shape[dim] - width, cells.shape[dim], axis=dim)
        cells = jnp.concatenate(
            [
                lax.ppermute(tail, axis, [(i, (i + 1) % count) for i in range(ends)]),
                cells,
                lax.ppermute(head, axis, [((i + 1) % count, i) for i in range(ends)]),
            ],
            axis=dim,
        )
    return cells


def packed_z_halo(fields, widths):
    width, size = max(widths), fields[0].shape[0]
    tails = jnp.concatenate([f[size - w :] for f, w in zip(fields, widths)], 0)
    heads = jnp.concatenate([f[:w] for f, w in zip(fields, widths)], 0)
    cells = jnp.stack(fields)
    from_below = from_behind(tails, "gz", 1)
    from_above = from_behind(heads, "gz", -1)
    cuts = [sum(widths[:i]) for i in range(len(widths) + 1)]
    below = jnp.stack(
        [
            jnp.pad(from_below[cuts[i] : cuts[i + 1]], ((width - w, 0), (0, 0), (0, 0)))
            for i, w in enumerate(widths)
        ]
    )
    above = jnp.stack(
        [
            jnp.pad(from_above[cuts[i] : cuts[i + 1]], ((0, width - w), (0, 0), (0, 0)))
            for i, w in enumerate(widths)
        ]
    )
    return jnp.concatenate((below, cells, above), axis=1)


def packed_z_fold(contributions, widths):
    width, size = max(widths), contributions.shape[1]
    lower = jnp.concatenate(
        [contributions[i, width - w : width] for i, w in enumerate(widths)], 0
    )
    upper = jnp.concatenate(
        [contributions[i, size - width : size - width + w] for i, w in enumerate(widths)], 0
    )
    lower, upper = lax.optimization_barrier((lower, upper))
    from_above = from_behind(lower, "gz", -1)
    from_below = from_behind(upper, "gz", 1)
    cuts = [sum(widths[:i]) for i in range(len(widths) + 1)]
    below = jnp.stack(
        [
            jnp.pad(from_below[cuts[i] : cuts[i + 1]], ((0, width - w), (0, 0), (0, 0)))
            for i, w in enumerate(widths)
        ]
    )
    above = jnp.stack(
        [
            jnp.pad(from_above[cuts[i] : cuts[i + 1]], ((width - w, 0), (0, 0), (0, 0)))
            for i, w in enumerate(widths)
        ]
    )
    middle = contributions[:, width : size - width]
    inner = size - 2 * width
    return jnp.concatenate(
        (
            middle[:, :width] + below,
            middle[:, width : inner - width],
            middle[:, inner - width :] + above,
        ),
        axis=1,
    )


def packed_y_halo(cells):
    depth, rows = cells.shape[1], cells.shape[2]

    def rims(lo, hi, narrow):
        return jnp.concatenate(
            (
                cells[0, :, lo:hi],
                jnp.concatenate(
                    (cells[1, 2 : depth - 2, narrow], cells[2, 2 : depth - 2, narrow]), axis=1
                ),
            ),
            axis=0,
        )

    lower = rims(0, 4, slice(0, 2))
    upper = rims(rows - 4, rows, slice(rows - 2, rows))
    lower, upper = lax.optimization_barrier((lower, upper))
    from_above = from_behind(lower, "gy", -1)
    from_below = from_behind(upper, "gy", 1)

    def unpack(arrived, outer):
        narrow = arrived[depth:]
        spread = ((2, 2), outer, (0, 0))
        return jnp.stack(
            (
                arrived[:depth],
                jnp.pad(narrow[:, :2], spread),
                jnp.pad(narrow[:, 2:], spread),
            )
        )

    return jnp.concatenate(
        (unpack(from_below, (2, 0)), cells, unpack(from_above, (0, 2))), axis=2
    )


def packed_y_fold(contributions):
    depth, rows = contributions.shape[1], contributions.shape[2]
    quarter = (depth - 4) // 4

    def rims(second_rows, third_first, third_second):
        second = contributions[1, 1 : depth - 1, second_rows]
        third = contributions[2, 2 : depth - 2]
        first_row = third[:, third_first : third_first + 1]
        second_row = jnp.pad(third[:, third_second : third_second + 1], ((1, 1), (0, 0), (0, 0)))
        return jnp.concatenate(
            (
                jnp.concatenate((second, second_row), axis=1),
                jnp.concatenate(
                    [first_row[k * quarter : (k + 1) * quarter] for k in range(4)], axis=1
                ),
            ),
            axis=0,
        )

    lower = jnp.concatenate(
        (contributions[0, :, 0:4], rims(slice(1, 4), 2, 3)), axis=0
    )
    upper = jnp.concatenate(
        (contributions[0, :, rows - 4 :], rims(slice(rows - 4, rows - 1), rows - 4, rows - 3)),
        axis=0,
    )
    lower, upper = lax.optimization_barrier((lower, upper))
    from_above = from_behind(lower, "gy", -1)
    from_below = from_behind(upper, "gy", 1)

    def unpack(arrived, second_side, third_side):
        block = arrived[depth : 2 * depth - 2]
        spread = arrived[2 * depth - 2 :]
        second = jnp.pad(block[:, 0:3], ((1, 1), second_side, (0, 0)))
        first_row = jnp.concatenate([spread[:, k : k + 1] for k in range(4)], axis=0)
        third = jnp.concatenate((first_row, block[1 : depth - 3, 3:4]), axis=1)
        third = jnp.pad(third, ((2, 2), third_side, (0, 0)))
        return jnp.stack((arrived[:depth], second, third))

    middle = contributions[:, :, 4 : rows - 4]
    return jnp.concatenate(
        (
            middle[:, :, :4] + unpack(from_below, (0, 1), (0, 2)),
            middle[:, :, 4:-4],
            middle[:, :, -4:] + unpack(from_above, (1, 0), (2, 0)),
        ),
        axis=2,
    )


def advance_solver_step(phase_wide, temp_wide, kinetic_rate_field):
    padded = jnp.pad(phase_wide, ((0, 0), (0, 0), (2, 2)))
    grad_z = 0.5 * (padded[2:, 1:-1, 1:-1] - padded[:-2, 1:-1, 1:-1])
    grad_y = 0.5 * (padded[1:-1, 2:, 1:-1] - padded[1:-1, :-2, 1:-1])
    grad_x = 0.5 * (padded[1:-1, 1:-1, 2:] - padded[1:-1, 1:-1, :-2])
    sq_z = grad_z * grad_z
    sq_y = grad_y * grad_y
    sq_x = grad_x * grad_x
    squared = sq_z + sq_y + sq_x + GRAD_FLOOR
    quartic = (sq_z * sq_z + sq_y * sq_y + sq_x * sq_x) / (squared * squared)
    anisotropy = 1.0 + ANISOTROPY * (4.0 * quartic - 3.0)
    aniso_sq = anisotropy * anisotropy
    factor_a = 16.0 * ANISOTROPY * anisotropy / squared
    flux_z = ENERGY_SCALE * (aniso_sq * grad_z + factor_a * grad_z * (sq_z - quartic * squared))
    flux_y = ENERGY_SCALE * (aniso_sq * grad_y + factor_a * grad_y * (sq_y - quartic * squared))
    flux_x = ENERGY_SCALE * (aniso_sq * grad_x + factor_a * grad_x * (sq_x - quartic * squared))
    divergence = 0.5 * (flux_z[2:, 1:-1, 1:-1] - flux_z[:-2, 1:-1, 1:-1])
    divergence = divergence + 0.5 * (flux_y[1:-1, 2:, 1:-1] - flux_y[1:-1, :-2, 1:-1])
    divergence = divergence + 0.5 * (flux_x[1:-1, 1:-1, 2:] - flux_x[1:-1, 1:-1, :-2])
    phase_now = phase_wide[2:-2, 2:-2]
    temp_now = temp_wide[2:-2, 2:-2]
    driving = DRIVE_SCALE / jnp.pi * jnp.arctan(DRIVE_SHARP * (MELT_POINT - temp_now))
    growth = kinetic_rate_field * (
        divergence + phase_now * (1.0 - phase_now) * (phase_now - 0.5 + driving)
    )
    new_phase = phase_now + TIME_STEP * growth
    temp_x = jnp.pad(temp_now, ((0, 0), (0, 0), (1, 1)))
    laplacian = (
        temp_wide[3:-1, 2:-2]
        + temp_wide[1:-3, 2:-2]
        + temp_wide[2:-2, 3:-1]
        + temp_wide[2:-2, 1:-3]
    )
    laplacian = laplacian + temp_x[:, :, 2:] + temp_x[:, :, :-2] - 6.0 * temp_now
    new_temp = temp_now + TIME_STEP * laplacian + LATENT_HEAT * (new_phase - phase_now)
    return (new_phase, new_temp)


def fold_rims(contributions, width, sides):
    for axis, dim in sides:
        size = contributions.shape[dim]
        lower_rim = lax.slice_in_dim(contributions, 0, width, axis=dim)
        upper_rim = lax.slice_in_dim(contributions, size - width, size, axis=dim)
        middle = lax.slice_in_dim(contributions, width, size - width, axis=dim)
        inner = size - 2 * width
        lower_rim, upper_rim = lax.optimization_barrier((lower_rim, upper_rim))
        from_above = from_behind(lower_rim, axis, -1)
        from_below = from_behind(upper_rim, axis, 1)
        contributions = jnp.concatenate(
            (
                lax.slice_in_dim(middle, 0, width, axis=dim) + from_below,
                lax.slice_in_dim(middle, width, inner - width, axis=dim),
                lax.slice_in_dim(middle, inner - width, inner, axis=dim) + from_above,
            ),
            axis=dim,
        )
    return contributions


def inside_grid(cells, margin):
    nz, ny = cells.shape[0] - 2 * margin, cells.shape[1] - 2 * margin
    z = lax.axis_index("gz") * nz - margin + lax.broadcasted_iota(jnp.int32, cells.shape, 0)
    y = lax.axis_index("gy") * ny - margin + lax.broadcasted_iota(jnp.int32, cells.shape, 1)
    total_z = nz * lax.axis_size("gz")
    total_y = ny * lax.axis_size("gy")
    return (z >= 0) & (z < total_z) & (y >= 0) & (y < total_y)


def body(
    saved_order_parameter,
    saved_heat_level,
    kinetic_rate_field,
    order_parameter_adjoint_seed,
    heat_level_adjoint_seed,
):
    state = packed_z_halo(
        (saved_order_parameter, saved_heat_level, kinetic_rate_field), (4, 2, 2)
    )
    state = packed_y_halo(state)
    phase_wide, temp_wide, rate_wide = state[0], state[1], state[2]
    succeeding_order_parameter, succeeding_heat_level = advance_solver_step(
        phase_wide, temp_wide, rate_wide[2:-2, 2:-2]
    )
    valid = inside_grid(succeeding_order_parameter, 2)
    discarded_result, sensitivity_latest = jax.vjp(
        advance_solver_step,
        succeeding_order_parameter,
        succeeding_heat_level,
        rate_wide[4:-4, 4:-4],
    )
    halfway_order_parameter, halfway_heat_level, latest_kinetic_rate = sensitivity_latest(
        (order_parameter_adjoint_seed, heat_level_adjoint_seed)
    )
    halfway_heat_level = jnp.where(valid, halfway_heat_level, 0.0)
    discarded_result, prior_backward_sweep = jax.vjp(
        advance_solver_step, phase_wide, temp_wide, rate_wide[2:-2, 2:-2]
    )
    sensitivity_order_parameter, sensitivity_heat_level, early_mob = prior_backward_sweep(
        (halfway_order_parameter, halfway_heat_level)
    )
    early_mob = early_mob.at[2:-2, 2:-2].add(latest_kinetic_rate)
    early_mob = jnp.pad(early_mob, ((2, 2), (2, 2), (0, 0)))
    folded = packed_y_fold(
        jnp.stack((sensitivity_order_parameter, sensitivity_heat_level, early_mob))
    )
    folded = packed_z_fold(folded, (4, 3, 2))
    return (folded[0], folded[1], folded[2])


def solution(mesh):
    return jax.shard_map(
        body,
        mesh=mesh,
        in_specs=(
            P("gz", "gy", None),
            P("gz", "gy", None),
            P("gz", "gy", None),
            P("gz", "gy", None),
            P("gz", "gy", None),
        ),
        out_specs=(P("gz", "gy", None), P("gz", "gy", None), P("gz", "gy", None)),
        check_vma=False,
    )
```

```python
import jax
import jax.numpy as jnp
from jax import lax
from jax.sharding import PartitionSpec as P

TIME_STEP = 0.15
ENERGY_SCALE = 0.5
ANISOTROPY = 0.05
GRAD_FLOOR = 0.01
LATENT_HEAT = 1.8
DRIVE_SCALE = 0.9
DRIVE_SHARP = 10.0
MELT_POINT = 1.0


def from_behind(block, axis, distance):
    devices = range(lax.axis_size(axis))
    route = [(i - distance, i) for i in devices if i - distance in devices]
    return lax.ppermute(block, axis, route)


def extended(cells, sides, width):
    for axis, dim in sides:
        count = lax.axis_size(axis)
        ends = count - 1
        head = lax.slice_in_dim(cells, 0, width, axis=dim)
        tail = lax.slice_in_dim(cells, cells.shape[dim] - width, cells.shape[dim], axis=dim)
        cells = jnp.concatenate(
            [
                lax.ppermute(tail, axis, [(i, (i + 1) % count) for i in range(ends)]),
                cells,
                lax.ppermute(head, axis, [((i + 1) % count, i) for i in range(ends)]),
            ],
            axis=dim,
        )
    return cells


def packed_z_halo(fields, widths):
    width, size = max(widths), fields[0].shape[0]
    tails = jnp.concatenate([f[size - w :] for f, w in zip(fields, widths)], 0)
    heads = jnp.concatenate([f[:w] for f, w in zip(fields, widths)], 0)
    cells = jnp.stack(fields)
    from_below = from_behind(tails, "gz", 1)
    from_above = from_behind(heads, "gz", -1)
    cuts = [sum(widths[:i]) for i in range(len(widths) + 1)]
    below = jnp.stack(
        [
            jnp.pad(from_below[cuts[i] : cuts[i + 1]], ((width - w, 0), (0, 0), (0, 0)))
            for i, w in enumerate(widths)
        ]
    )
    above = jnp.stack(
        [
            jnp.pad(from_above[cuts[i] : cuts[i + 1]], ((0, width - w), (0, 0), (0, 0)))
            for i, w in enumerate(widths)
        ]
    )
    return jnp.concatenate((below, cells, above), axis=1)


def packed_z_fold(contributions, widths):
    width, size = max(widths), contributions.shape[1]
    lower = jnp.concatenate(
        [contributions[i, width - w : width] for i, w in enumerate(widths)], 0
    )
    upper = jnp.concatenate(
        [contributions[i, size - width : size - width + w] for i, w in enumerate(widths)], 0
    )
    lower, upper = lax.optimization_barrier((lower, upper))
    from_above = from_behind(lower, "gz", -1)
    from_below = from_behind(upper, "gz", 1)
    cuts = [sum(widths[:i]) for i in range(len(widths) + 1)]
    below = jnp.stack(
        [
            jnp.pad(from_below[cuts[i] : cuts[i + 1]], ((0, width - w), (0, 0), (0, 0)))
            for i, w in enumerate(widths)
        ]
    )
    above = jnp.stack(
        [
            jnp.pad(from_above[cuts[i] : cuts[i + 1]], ((width - w, 0), (0, 0), (0, 0)))
            for i, w in enumerate(widths)
        ]
    )
    middle = contributions[:, width : size - width]
    inner = size - 2 * width
    return jnp.concatenate(
        (
            middle[:, :width] + below,
            middle[:, width : inner - width],
            middle[:, inner - width :] + above,
        ),
        axis=1,
    )


def packed_y_halo(cells):
    depth, rows = cells.shape[1], cells.shape[2]

    def rims(lo, hi, narrow):
        return jnp.concatenate(
            (
                cells[0, :, lo:hi],
                jnp.concatenate(
                    (cells[1, 2 : depth - 2, narrow], cells[2, 2 : depth - 2, narrow]), axis=1
                ),
            ),
            axis=0,
        )

    lower = rims(0, 4, slice(0, 2))
    upper = rims(rows - 4, rows, slice(rows - 2, rows))
    from_above = from_behind(lower, "gy", -1)
    from_below = from_behind(upper, "gy", 1)

    def unpack(arrived, outer):
        narrow = arrived[depth:]
        spread = ((2, 2), outer, (0, 0))
        return jnp.stack(
            (
                arrived[:depth],
                jnp.pad(narrow[:, :2], spread),
                jnp.pad(narrow[:, 2:], spread),
            )
        )

    return jnp.concatenate(
        (unpack(from_below, (2, 0)), cells, unpack(from_above, (0, 2))), axis=2
    )


def packed_y_fold(contributions):
    depth, rows = contributions.shape[1], contributions.shape[2]
    quarter = (depth - 4) // 4

    def rims(second_rows, third_first, third_second):
        second = contributions[1, 1 : depth - 1, second_rows]
        third = contributions[2, 2 : depth - 2]
        first_row = third[:, third_first : third_first + 1]
        second_row = jnp.pad(third[:, third_second : third_second + 1], ((1, 1), (0, 0), (0, 0)))
        return jnp.concatenate(
            (
                jnp.concatenate((second, second_row), axis=1),
                jnp.concatenate(
                    [first_row[k * quarter : (k + 1) * quarter] for k in range(4)], axis=1
                ),
            ),
            axis=0,
        )

    lower = jnp.concatenate(
        (contributions[0, :, 0:4], rims(slice(1, 4), 2, 3)), axis=0
    )
    upper = jnp.concatenate(
        (contributions[0, :, rows - 4 :], rims(slice(rows - 4, rows - 1), rows - 4, rows - 3)),
        axis=0,
    )
    lower, upper = lax.optimization_barrier((lower, upper))
    from_above = from_behind(lower, "gy", -1)
    from_below = from_behind(upper, "gy", 1)

    def unpack(arrived, second_side, third_side):
        block = arrived[depth : 2 * depth - 2]
        spread = arrived[2 * depth - 2 :]
        second = jnp.pad(block[:, 0:3], ((1, 1), second_side, (0, 0)))
        first_row = jnp.concatenate([spread[:, k : k + 1] for k in range(4)], axis=0)
        third = jnp.concatenate((first_row, block[1 : depth - 3, 3:4]), axis=1)
        third = jnp.pad(third, ((2, 2), third_side, (0, 0)))
        return jnp.stack((arrived[:depth], second, third))

    middle = contributions[:, :, 4 : rows - 4]
    return jnp.concatenate(
        (
            middle[:, :, :4] + unpack(from_below, (0, 1), (0, 2)),
            middle[:, :, 4:-4],
            middle[:, :, -4:] + unpack(from_above, (1, 0), (2, 0)),
        ),
        axis=2,
    )


def advance_solver_step(phase_wide, temp_wide, kinetic_rate_field):
    padded = jnp.pad(phase_wide, ((0, 0), (0, 0), (2, 2)))
    grad_z = 0.5 * (padded[2:, 1:-1, 1:-1] - padded[:-2, 1:-1, 1:-1])
    grad_y = 0.5 * (padded[1:-1, 2:, 1:-1] - padded[1:-1, :-2, 1:-1])
    grad_x = 0.5 * (padded[1:-1, 1:-1, 2:] - padded[1:-1, 1:-1, :-2])
    sq_z = grad_z * grad_z
    sq_y = grad_y * grad_y
    sq_x = grad_x * grad_x
    squared = sq_z + sq_y + sq_x + GRAD_FLOOR
    quartic = (sq_z * sq_z + sq_y * sq_y + sq_x * sq_x) / (squared * squared)
    anisotropy = 1.0 + ANISOTROPY * (4.0 * quartic - 3.0)
    aniso_sq = anisotropy * anisotropy
    factor_a = 16.0 * ANISOTROPY * anisotropy / squared
    flux_z = ENERGY_SCALE * (aniso_sq * grad_z + factor_a * grad_z * (sq_z - quartic * squared))
    flux_y = ENERGY_SCALE * (aniso_sq * grad_y + factor_a * grad_y * (sq_y - quartic * squared))
    flux_x = ENERGY_SCALE * (aniso_sq * grad_x + factor_a * grad_x * (sq_x - quartic * squared))
    divergence = 0.5 * (flux_z[2:, 1:-1, 1:-1] - flux_z[:-2, 1:-1, 1:-1])
    divergence = divergence + 0.5 * (flux_y[1:-1, 2:, 1:-1] - flux_y[1:-1, :-2, 1:-1])
    divergence = divergence + 0.5 * (flux_x[1:-1, 1:-1, 2:] - flux_x[1:-1, 1:-1, :-2])
    phase_now = phase_wide[2:-2, 2:-2]
    temp_now = temp_wide[2:-2, 2:-2]
    driving = DRIVE_SCALE / jnp.pi * jnp.arctan(DRIVE_SHARP * (MELT_POINT - temp_now))
    growth = kinetic_rate_field * (
        divergence + phase_now * (1.0 - phase_now) * (phase_now - 0.5 + driving)
    )
    new_phase = phase_now + TIME_STEP * growth
    temp_x = jnp.pad(temp_now, ((0, 0), (0, 0), (1, 1)))
    laplacian = (
        temp_wide[3:-1, 2:-2]
        + temp_wide[1:-3, 2:-2]
        + temp_wide[2:-2, 3:-1]
        + temp_wide[2:-2, 1:-3]
    )
    laplacian = laplacian + temp_x[:, :, 2:] + temp_x[:, :, :-2] - 6.0 * temp_now
    new_temp = temp_now + TIME_STEP * laplacian + LATENT_HEAT * (new_phase - phase_now)
    return (new_phase, new_temp)


def fold_rims(contributions, width, sides):
    for axis, dim in sides:
        size = contributions.shape[dim]
        lower_rim = lax.slice_in_dim(contributions, 0, width, axis=dim)
        upper_rim = lax.slice_in_dim(contributions, size - width, size, axis=dim)
        middle = lax.slice_in_dim(contributions, width, size - width, axis=dim)
        inner = size - 2 * width
        lower_rim, upper_rim = lax.optimization_barrier((lower_rim, upper_rim))
        from_above = from_behind(lower_rim, axis, -1)
        from_below = from_behind(upper_rim, axis, 1)
        contributions = jnp.concatenate(
            (
                lax.slice_in_dim(middle, 0, width, axis=dim) + from_below,
                lax.slice_in_dim(middle, width, inner - width, axis=dim),
                lax.slice_in_dim(middle, inner - width, inner, axis=dim) + from_above,
            ),
            axis=dim,
        )
    return contributions


def inside_grid(cells, margin):
    nz, ny = cells.shape[0] - 2 * margin, cells.shape[1] - 2 * margin
    z = lax.axis_index("gz") * nz - margin + lax.broadcasted_iota(jnp.int32, cells.shape, 0)
    y = lax.axis_index("gy") * ny - margin + lax.broadcasted_iota(jnp.int32, cells.shape, 1)
    total_z = nz * lax.axis_size("gz")
    total_y = ny * lax.axis_size("gy")
    return (z >= 0) & (z < total_z) & (y >= 0) & (y < total_y)


def body(
    saved_order_parameter,
    saved_heat_level,
    kinetic_rate_field,
    order_parameter_adjoint_seed,
    heat_level_adjoint_seed,
):
    state = packed_z_halo(
        (saved_order_parameter, saved_heat_level, kinetic_rate_field), (4, 2, 2)
    )
    state = packed_y_halo(state)
    phase_wide, temp_wide, rate_wide = state[0], state[1], state[2]
    succeeding_order_parameter, succeeding_heat_level = advance_solver_step(
        phase_wide, temp_wide, rate_wide[2:-2, 2:-2]
    )
    valid = inside_grid(succeeding_order_parameter, 2)
    discarded_result, sensitivity_latest = jax.vjp(
        advance_solver_step,
        succeeding_order_parameter,
        succeeding_heat_level,
        rate_wide[4:-4, 4:-4],
    )
    halfway_order_parameter, halfway_heat_level, latest_kinetic_rate = sensitivity_latest(
        (order_parameter_adjoint_seed, heat_level_adjoint_seed)
    )
    halfway_heat_level = jnp.where(valid, halfway_heat_level, 0.0)
    discarded_result, prior_backward_sweep = jax.vjp(
        advance_solver_step, phase_wide, temp_wide, rate_wide[2:-2, 2:-2]
    )
    sensitivity_order_parameter, sensitivity_heat_level, early_mob = prior_backward_sweep(
        (halfway_order_parameter, halfway_heat_level)
    )
    early_mob = jnp.pad(early_mob, ((2, 2), (2, 2), (0, 0)))
    folded = packed_y_fold(
        jnp.stack((sensitivity_order_parameter, sensitivity_heat_level, early_mob))
    )
    folded = packed_z_fold(folded, (4, 3, 2))
    return (folded[0], folded[1], latest_kinetic_rate + folded[2])


def solution(mesh):
    return jax.shard_map(
        body,
        mesh=mesh,
        in_specs=(
            P("gz", "gy", None),
            P("gz", "gy", None),
            P("gz", "gy", None),
            P("gz", "gy", None),
            P("gz", "gy", None),
        ),
        out_specs=(P("gz", "gy", None), P("gz", "gy", None), P("gz", "gy", None)),
        check_vma=False,
    )
```
